256 devices in a mesh: in: 4 (over x), out: 64 (over z, y, core).
Axes of the slice: x: 4, y: 4, z: 8, core: 2. Of those that a mesh axis runs over, the one named last changes fastest.
Arguments:
- activations: bfloat16 [8192, 4096], P('out', 'in'), may hold values from -6 to 6
- out_grad: bfloat16 [8192, 16384], P('in', 'out'), may hold values from -0.06591797 to 0.06591797
- block_rows: int32 [4, 64, 4], P('in', 'out'), may hold values from 0 to 31, as said below
- block_cols: int32 [4, 64, 4], P('in', 'out'), may hold values from 0 to 127, as said below
- counts: int32 [4, 64], P('in', 'out'), may hold values from 1 to 4, as said below
Outputs:
- grad_blocks: float32 [4, 64, 4, 128, 128], P('in', 'out')
The draws below stay inside these ranges and needn't reach their ends.
Inputs may be any that keep to these rules, and one draw needn't show every extreme that they name: `block_rows`: tile (i, j) lists blocks of its own region only: rows i * 8 to (i + 1) * 8 - 1; slots of one tile name different blocks, and slots past counts[i, j] also name blocks of the tile. `block_cols`: columns j * 2 to (j + 1) * 2 - 1 for tile (i, j). `counts`: some tile has a full list in every draw.
All inputs are finite; a program needn't handle non-finite values.
Results may differ from the reference program's by a relative error of at most 0.0003.
Values may be sent and summed in bfloat16 or wider, within the bound.
No kernel may reach another device: no remote copies, remote signals or barrier semaphores. Data moves between devices by JAX's collectives and lax.ppermute only.
A program may use at most 128 MiB of HBM per device.

```python
import jax
import jax.numpy as jnp
from jax import lax

D = 4096
FFW = 16384
BLK = 128
MAXB = 4
TOKENS = 8192
NBR = 32
NBC = 128
TBR = 8
TBC = 2
N_IN = 4
N_OUT = 64


def block_lists(key):
    base = jax.random.fold_in(key, 11)
    tile_keys = jax.random.split(base, N_IN * N_OUT)

    def one_tile(tile_key):
        return jax.random.permutation(tile_key, TBR * TBC)[:MAXB]
    picked = jax.vmap(one_tile)(tile_keys).reshape(N_IN, N_OUT, MAXB).astype(jnp.int32)
    in_index = jnp.arange(N_IN, dtype=jnp.int32)[:, None, None]
    out_index = jnp.arange(N_OUT, dtype=jnp.int32)[None, :, None]
    rows_global = picked // TBC + in_index * TBR
    cols_global = picked % TBC + out_index * TBC
    return (rows_global, cols_global)


def draw_block_rows(key, part):
    return block_lists(key)[0].astype(jnp.int32)


def draw_block_cols(key, part):
    return block_lists(key)[1].astype(jnp.int32)


def draw_counts(key, part):
    base = jax.random.fold_in(key, 23)
    first_key, second_key, third_key = jax.random.split(base, 3)
    first = jax.random.randint(first_key, (N_IN * N_OUT,), 1, MAXB + 1)
    second = jax.random.randint(second_key, (N_IN * N_OUT,), 1, MAXB + 1)
    smaller = jnp.minimum(first, second)
    full_tile = jax.random.randint(third_key, (), 0, N_IN * N_OUT)
    slots = jnp.arange(N_IN * N_OUT, dtype=jnp.int32)
    filled = jnp.where(slots == full_tile, MAXB, smaller)
    return filled.reshape(N_IN, N_OUT).astype(jnp.int32)


def block_levels(own_key, shape, cuts, low, high):
    loudness, own = 1.0, jax.random.fold_in(own_key, 6)
    for dim, blocks in cuts:
        heights = jnp.exp(jax.random.uniform(jax.random.fold_in(own, dim), (blocks,), jnp.float32, low / len(cuts), high / len(cuts)))
        loudness = loudness * jnp.repeat(heights, shape[dim] // blocks).reshape([-1 if axis == dim else 1 for axis in range(len(shape))])
    return loudness


def scatter_about(stream_key, extent, spread, limit, pieces=(), kind=jnp.bfloat16):
    drawn = spread * jax.random.normal(stream_key, extent, jnp.float32)
    if pieces:
        drawn = drawn * block_levels(stream_key, extent, pieces, -0.22, 0.18)
    return jnp.clip(drawn, -limit, limit).astype(kind)


def setup_inputs(seed: int = 0) -> dict:
    key_of = jax.random.split(jax.random.key(seed), 6)
    return {
        "activations": scatter_about(key_of[0], (TOKENS, D), 1.0, 6.0, ((0, 64), (1, 4))),
        "out_grad": scatter_about(key_of[1], (TOKENS, FFW), (1.0 / TOKENS ** 0.5), 0.06591797, ((0, 4), (1, 64))),
        "block_rows": draw_block_rows(jax.random.fold_in(key_of[5], 71), 0),
        "block_cols": draw_block_cols(jax.random.fold_in(key_of[5], 71), 0),
        "counts": draw_counts(jax.random.fold_in(key_of[5], 71), 0),
    }


def reference(activations, out_grad, block_rows, block_cols, counts):
    act_blocks = activations.astype(jnp.float32).reshape(TOKENS, NBR, BLK)
    grad_cols = out_grad.astype(jnp.float32).reshape(TOKENS, NBC, BLK)
    rows_flat = block_rows.reshape(N_IN * N_OUT, MAXB)
    cols_flat = block_cols.reshape(N_IN * N_OUT, MAXB)
    count_flat = counts.reshape(N_IN * N_OUT)

    def one_tile(entry):
        rows_here, cols_here, live = entry
        left = jnp.take(act_blocks, rows_here, axis=1)
        right = jnp.take(grad_cols, cols_here, axis=1)
        blocks = jnp.einsum("tbi,tbj->bij", left, right, precision=lax.Precision.HIGHEST)
        keep = (jnp.arange(MAXB, dtype=jnp.int32) < live)[:, None, None]
        return jnp.where(keep, blocks, jnp.zeros_like(blocks))

    tiles = lax.map(one_tile, (rows_flat, cols_flat, count_flat))
    return tiles.reshape(N_IN, N_OUT, MAXB, BLK, BLK)
```

```python
import functools

import jax
import jax.numpy as jnp
from jax import lax
from jax.experimental import pallas as pl
from jax.experimental.pallas import tpu as pltpu
from jax.sharding import PartitionSpec as P

BLK = 128
MAXB = 4
CHUNK = 512


def block_kernel(n_grad, rows_ref, cols_ref, live_ref, starts_ref, act_hbm, *rest):
    grad_hbm = rest[:n_grad]
    out_ref, a_v, g_v, sems = rest[n_grad:]
    tokens = a_v.shape[1]

    copies = []
    for s in range(MAXB):
        r = pl.multiple_of(rows_ref[s] * BLK, BLK)
        c = pl.multiple_of(cols_ref[s] * BLK, BLK)
        slot = [pltpu.make_async_copy(act_hbm.at[:, pl.ds(r, BLK)], a_v.at[s], sems.at[s, 0])]
        for p, piece in enumerate(grad_hbm):
            length = piece.shape[0]
            slot.append(
                pltpu.make_async_copy(
                    piece.at[:, pl.ds(c, BLK)],
                    g_v.at[s, pl.ds(pl.multiple_of(starts_ref[p], BLK), length)],
                    sems.at[s, p + 1],
                )
            )
        for cp in slot:
            cp.start()
        copies.append(slot)

    live = live_ref[0]
    for s in range(MAXB):
        for cp in copies[s]:
            cp.wait()

        def body(k, acc):
            t = pl.multiple_of(k * CHUNK, CHUNK)
            a = a_v[s, pl.ds(t, CHUNK), :]
            g = g_v[s, pl.ds(t, CHUNK), :]
            return acc + lax.dot_general(
                a, g, (((0,), (0,)), ((), ())), preferred_element_type=jnp.float32
            )

        acc = lax.fori_loop(0, tokens // CHUNK, body, jnp.zeros((BLK, BLK), jnp.float32))
        out_ref[s] = jnp.where(s < live, acc, jnp.zeros_like(acc))


def block_products(act_all, grad_pieces, starts, local_rows, local_cols, live):
    tokens = act_all.shape[0]
    n_grad = len(grad_pieces)
    smem = pl.BlockSpec(memory_space=pltpu.SMEM)
    hbm = pl.BlockSpec(memory_space=pl.ANY)
    flops = 2 * MAXB * tokens * BLK * BLK
    moved = 2 * MAXB * tokens * BLK * 2 + MAXB * BLK * BLK * 4
    return pl.pallas_call(
        functools.partial(block_kernel, n_grad),
        out_shape=jax.ShapeDtypeStruct((MAXB, BLK, BLK), jnp.float32),
        in_specs=[smem, smem, smem, smem, hbm] + [hbm] * n_grad,
        out_specs=pl.BlockSpec(memory_space=pltpu.VMEM),
        scratch_shapes=[
            pltpu.VMEM((MAXB, tokens, BLK), jnp.bfloat16),
            pltpu.VMEM((MAXB, tokens, BLK), jnp.bfloat16),
            pltpu.SemaphoreType.DMA((MAXB, 1 + n_grad)),
        ],
        compiler_params=pltpu.CompilerParams(vmem_limit_bytes=48 * 1024 * 1024),
        cost_estimate=pl.CostEstimate(flops=flops, bytes_accessed=moved, transcendentals=0),
    )(local_rows, local_cols, live, starts, act_all, *grad_pieces)


def ring_gather(own, axis, place):
    n = lax.axis_size(axis)
    length = own.shape[0]
    right = [(k, (k + 1) % n) for k in range(n)]
    left = [(k, (k - 1) % n) for k in range(n)]
    pieces, starts = [own], [place * length]
    from_left, from_right = own, own
    for d in range(1, (n + 1) // 2):
        from_left = lax.ppermute(from_left, axis, right)
        from_right = lax.ppermute(from_right, axis, left)
        pieces += [from_left, from_right]
        starts += [((place - d) % n) * length, ((place + d) % n) * length]
    if n % 2 == 0 and n > 1:
        half = length // 2
        d = n // 2
        if d == 1:
            near_a, near_b = lax.ppermute(own[:half], axis, right), lax.ppermute(own[half:], axis, left)
        else:
            near_a = lax.ppermute(from_left[:half], axis, right)
            near_b = lax.ppermute(from_right[half:], axis, left)
        far = ((place + d) % n) * length
        pieces += [near_a, near_b]
        starts += [far, far + half]
    return pieces, jnp.stack(starts).astype(jnp.int32)


def on_device(activations, out_grad, block_rows, block_cols, counts):
    in_place = lax.axis_index("in")
    out_place = lax.axis_index("out")
    tile_rows = activations.shape[1] // BLK
    tile_cols = out_grad.shape[1] // BLK
    local_rows = jnp.clip(block_rows[0, 0] - in_place * tile_rows, 0, tile_rows - 1)
    local_cols = jnp.clip(block_cols[0, 0] - out_place * tile_cols, 0, tile_cols - 1)
    live = counts[0].astype(jnp.int32)
    act_all = lax.all_gather(activations, "out", axis=0, tiled=True)
    grad_pieces, starts = ring_gather(out_grad, "in", in_place)
    totals = block_products(act_all, grad_pieces, starts, local_rows, local_cols, live)
    return totals.reshape(1, 1, MAXB, BLK, BLK)


def solution(mesh):
    return jax.shard_map(
        on_device,
        mesh=mesh,
        in_specs=(
            P("out", "in"),
            P("in", "out"),
            P("in", "out", None),
            P("in", "out", None),
            P("in", "out"),
        ),
        out_specs=P("in", "out", None, None, None),
        check_vma=False,
    )
```

```python
import functools

import jax
import jax.numpy as jnp
from jax import lax
from jax.experimental import pallas as pl
from jax.experimental.pallas import tpu as pltpu
from jax.sharding import PartitionSpec as P

BLK = 128
MAXB = 4
CHUNK = 512


def block_kernel(n_grad, rows_ref, cols_ref, use_ref, starts_ref, act_hbm, *rest):
    grad_hbm = rest[:n_grad]
    out_ref, a_v, g_v, sems = rest[n_grad:]
    tokens = a_v.shape[1]

    copies = []
    for s in range(MAXB):
        r = pl.multiple_of(rows_ref[s] * BLK, BLK)
        c = pl.multiple_of(cols_ref[s] * BLK, BLK)
        slot = [pltpu.make_async_copy(act_hbm.at[:, pl.ds(r, BLK)], a_v.at[s], sems.at[s, 0])]
        for p, piece in enumerate(grad_hbm):
            length = piece.shape[0]
            slot.append(
                pltpu.make_async_copy(
                    piece.at[:, pl.ds(c, BLK)],
                    g_v.at[s, pl.ds(pl.multiple_of(starts_ref[p], BLK), length)],
                    sems.at[s, p + 1],
                )
            )

        @pl.when(use_ref[s] == 1)
        def _(slot=slot):
            for cp in slot:
                cp.start()

        copies.append(slot)

    for s in range(MAXB):

        @pl.when(use_ref[s] == 0)
        def _(s=s):
            out_ref[s] = jnp.zeros((BLK, BLK), jnp.float32)

        @pl.when(use_ref[s] == 1)
        def _(s=s):
            slot_products(s, copies[s], a_v, g_v, out_ref, tokens)


def slot_products(s, slot, a_v, g_v, out_ref, tokens):
    for cp in slot:
        cp.wait()

    def body(k, acc):
        t = pl.multiple_of(k * CHUNK, CHUNK)
        a = a_v[s, pl.ds(t, CHUNK), :]
        g = g_v[s, pl.ds(t, CHUNK), :]
        return acc + lax.dot_general(
            a, g, (((0,), (0,)), ((), ())), preferred_element_type=jnp.float32
        )

    out_ref[s] = lax.fori_loop(0, tokens // CHUNK, body, jnp.zeros((BLK, BLK), jnp.float32))


def block_products(act_all, grad_pieces, starts, local_rows, local_cols, use):
    tokens = act_all.shape[0]
    n_grad = len(grad_pieces)
    smem = pl.BlockSpec(memory_space=pltpu.SMEM)
    hbm = pl.BlockSpec(memory_space=pl.ANY)
    flops = 2 * MAXB * tokens * BLK * BLK
    moved = 2 * MAXB * tokens * BLK * 2 + MAXB * BLK * BLK * 4
    return pl.pallas_call(
        functools.partial(block_kernel, n_grad),
        out_shape=jax.ShapeDtypeStruct((MAXB, BLK, BLK), jnp.float32),
        in_specs=[smem, smem, smem, smem, hbm] + [hbm] * n_grad,
        out_specs=pl.BlockSpec(memory_space=pltpu.VMEM),
        scratch_shapes=[
            pltpu.VMEM((MAXB, tokens, BLK), jnp.bfloat16),
            pltpu.VMEM((MAXB, tokens, BLK), jnp.bfloat16),
            pltpu.SemaphoreType.DMA((MAXB, 1 + n_grad)),
        ],
        compiler_params=pltpu.CompilerParams(vmem_limit_bytes=48 * 1024 * 1024),
        cost_estimate=pl.CostEstimate(flops=flops, bytes_accessed=moved, transcendentals=0),
    )(local_rows, local_cols, use, starts, act_all, *grad_pieces)


def ring_gather(own, axis, place):
    n = lax.axis_size(axis)
    length = own.shape[0]
    right = [(k, (k + 1) % n) for k in range(n)]
    left = [(k, (k - 1) % n) for k in range(n)]
    pieces, starts = [own], [place * length]
    from_left, from_right = own, own
    for d in range(1, (n + 1) // 2):
        from_left = lax.ppermute(from_left, axis, right)
        from_right = lax.ppermute(from_right, axis, left)
        pieces += [from_left, from_right]
        starts += [((place - d) % n) * length, ((place + d) % n) * length]
    if n % 2 == 0 and n > 1:
        half = length // 2
        d = n // 2
        if d == 1:
            near_a, near_b = lax.ppermute(own[:half], axis, right), lax.ppermute(own[half:], axis, left)
        else:
            near_a = lax.ppermute(from_left[:half], axis, right)
            near_b = lax.ppermute(from_right[half:], axis, left)
        far = ((place + d) % n) * length
        pieces += [near_a, near_b]
        starts += [far, far + half]
    return pieces, jnp.stack(starts).astype(jnp.int32)


def on_device(activations, out_grad, block_rows, block_cols, counts):
    in_place = lax.axis_index("in")
    core = lax.axis_index("core")
    out_place = lax.axis_index("zy") * lax.axis_size("core") + core
    tile_rows = activations.shape[1] // BLK
    tile_cols = out_grad.shape[1] // BLK
    half_rows = tile_rows // 2
    local_rows = jnp.clip(block_rows[0, 0] - in_place * tile_rows, 0, tile_rows - 1)
    local_cols = jnp.clip(block_cols[0, 0] - out_place * tile_cols, 0, tile_cols - 1)
    live = jnp.arange(MAXB, dtype=jnp.int32) < counts[0, 0]
    mine_half = (local_rows // half_rows) == core
    use_mine = (live & mine_half).astype(jnp.int32)
    use_other = (live & ~mine_half).astype(jnp.int32)
    in_half = (local_rows % half_rows).astype(jnp.int32)

    width = half_rows * BLK
    first, second = activations[:, :width], activations[:, width:]
    on_first = core == 0
    keep = jnp.where(on_first, first, second)
    send = jnp.where(on_first, second, first)
    swap = [(0, 1), (1, 0)]
    recv = lax.ppermute(send, "core", swap)
    pair = jnp.where(
        on_first, jnp.concatenate([keep, recv], 0), jnp.concatenate([recv, keep], 0)
    )
    mine = lax.all_gather(pair, "zy", axis=0, tiled=True)
    grad_pieces, starts = ring_gather(out_grad, "in", in_place)
    mine, grad_pieces = lax.optimization_barrier((mine, grad_pieces))
    other = lax.ppermute(mine, "core", swap)
    part_mine = block_products(mine, grad_pieces, starts, in_half, local_cols, use_mine)
    part_other = block_products(other, grad_pieces, starts, in_half, local_cols, use_other)
    totals = part_mine + part_other
    return totals.reshape(1, 1, MAXB, BLK, BLK)


def solution(mesh):
    n_in, n_out = mesh.devices.shape
    split = jax.sharding.Mesh(mesh.devices.reshape(n_in, n_out // 2, 2), ("in", "zy", "core"))
    out = ("zy", "core")
    return jax.shard_map(
        on_device,
        mesh=split,
        in_specs=(
            P(out, "in"),
            P("in", out),
            P("in", out, None),
            P("in", out, None),
            P("in", out),
        ),
        out_specs=P("in", out, None, None, None),
        check_vma=False,
    )
```

```python
import functools

import jax
import jax.numpy as jnp
from jax import lax
from jax.experimental import pallas as pl
from jax.experimental.pallas import tpu as pltpu
from jax.sharding import PartitionSpec as P

BLK = 128
MAXB = 4


def block_kernel(n_grad, ny, rows_ref, cols_ref, use_ref, starts_ref, place_ref, *rest):
    first_hbm, second_hbm = rest[0], rest[1]
    grad_hbm = rest[2:2 + n_grad]
    out_ref, a_v, g_v, sems = rest[2 + n_grad:]
    chunks = a_v.shape[2]

    copies = []
    for s in range(MAXB):
        r = pl.multiple_of(rows_ref[s] * BLK, BLK)
        c = pl.multiple_of(cols_ref[s] * BLK, BLK)
        slot = [
            pltpu.make_async_copy(first_hbm.at[:, :, pl.ds(r, BLK)], a_v.at[s, 0], sems.at[s, 0]),
            pltpu.make_async_copy(second_hbm.at[:, :, pl.ds(r, BLK)], a_v.at[s, 1], sems.at[s, 1]),
        ]
        for p, piece in enumerate(grad_hbm):
            slot.append(
                pltpu.make_async_copy(
                    piece.at[:, :, :, pl.ds(c, BLK)],
                    g_v.at[s, pl.ds(starts_ref[p], piece.shape[0])],
                    sems.at[s, p + 2],
                )
            )

        @pl.when(use_ref[s] == 1)
        def _(slot=slot):
            for cp in slot:
                cp.start()

        copies.append(slot)

    z_me, y_me = place_ref[0], place_ref[1]
    nz = chunks // ny
    for s in range(MAXB):

        @pl.when(use_ref[s] == 0)
        def _(s=s):
            out_ref[s] = jnp.zeros((BLK, BLK), jnp.float32)

        @pl.when(use_ref[s] == 1)
        def _(s=s):
            for cp in copies[s]:
                cp.wait()

            def body(k, acc):
                pair = ((z_me + k // ny) % nz) * ny + (y_me + k % ny) % ny
                for half in range(2):
                    a = a_v[s, half, k]
                    g = g_v[s, pair, half]
                    acc = acc + lax.dot_general(
                        a, g, (((0,), (0,)), ((), ())), preferred_element_type=jnp.float32
                    )
                return acc

            out_ref[s] = lax.fori_loop(0, chunks, body, jnp.zeros((BLK, BLK), jnp.float32))


def block_products(first, second, grad_pieces, starts, place, local_rows, local_cols, use, ny):
    chunks, tok, width = first.shape
    n_grad = len(grad_pieces)
    smem = pl.BlockSpec(memory_space=pltpu.SMEM)
    hbm = pl.BlockSpec(memory_space=pl.ANY)
    tokens = 2 * chunks * tok
    flops = 2 * MAXB * tokens * BLK * BLK
    moved = 2 * MAXB * tokens * BLK * 2 + MAXB * BLK * BLK * 4
    return pl.pallas_call(
        functools.partial(block_kernel, n_grad, ny),
        out_shape=jax.ShapeDtypeStruct((MAXB, BLK, BLK), jnp.float32),
        in_specs=[smem] * 5 + [hbm] * (2 + n_grad),
        out_specs=pl.BlockSpec(memory_space=pltpu.VMEM),
        scratch_shapes=[
            pltpu.VMEM((MAXB, 2, chunks, tok, BLK), jnp.bfloat16),
            pltpu.VMEM((MAXB, chunks, 2, tok, BLK), jnp.bfloat16),
            pltpu.SemaphoreType.DMA((MAXB, 2 + n_grad)),
        ],
        compiler_params=pltpu.CompilerParams(vmem_limit_bytes=48 * 1024 * 1024),
        cost_estimate=pl.CostEstimate(flops=flops, bytes_accessed=moved, transcendentals=0),
    )(local_rows, local_cols, use, starts, place, first, second, *grad_pieces)


def relative_gather(x, axis, n):
    right = [(k, (k + 1) % n) for k in range(n)]
    left = [(k, (k - 1) % n) for k in range(n)]
    rel = [x] + [None] * (n - 1)
    from_left, from_right = x, x
    for t in range(1, (n + 1) // 2):
        from_left = lax.ppermute(from_left, axis, right)
        from_right = lax.ppermute(from_right, axis, left)
        rel[n - t] = from_left
        rel[t] = from_right
    if n % 2 == 0 and n > 1:
        t = n // 2
        half = x.shape[0] // 2
        near_a = lax.ppermute(from_left[:half], axis, right)
        near_b = lax.ppermute(from_right[half:], axis, left)
        rel[t] = jnp.concatenate([near_a, near_b], 0)
    return rel


def ring_gather(own, axis, place):
    n = lax.axis_size(axis)
    length = own.shape[0]
    right = [(k, (k + 1) % n) for k in range(n)]
    left = [(k, (k - 1) % n) for k in range(n)]
    pieces, starts = [own], [place * length]
    from_left, from_right = own, own
    for d in range(1, (n + 1) // 2):
        from_left = lax.ppermute(from_left, axis, right)
        from_right = lax.ppermute(from_right, axis, left)
        pieces += [from_left, from_right]
        starts += [((place - d) % n) * length, ((place + d) % n) * length]
    if n % 2 == 0 and n > 1:
        half = length // 2
        d = n // 2
        if d == 1:
            near_a, near_b = lax.ppermute(own[:half], axis, right), lax.ppermute(own[half:], axis, left)
        else:
            near_a = lax.ppermute(from_left[:half], axis, right)
            near_b = lax.ppermute(from_right[half:], axis, left)
        far = ((place + d) % n) * length
        pieces += [near_a, near_b]
        starts += [far, far + half]
    return pieces, jnp.stack(starts).astype(jnp.int32)


def on_device(activations, out_grad, block_rows, block_cols, counts):
    in_place = lax.axis_index("in")
    core = lax.axis_index("core")
    nz, ny, ncore = lax.axis_size("z"), lax.axis_size("y"), lax.axis_size("core")
    z_me, y_me = lax.axis_index("z"), lax.axis_index("y")
    out_place = (z_me * ny + y_me) * ncore + core
    tok = activations.shape[0]
    tile_rows = activations.shape[1] // BLK
    tile_cols = out_grad.shape[1] // BLK
    half_rows = tile_rows // 2
    local_rows = jnp.clip(block_rows[0, 0] - in_place * tile_rows, 0, tile_rows - 1)
    local_cols = jnp.clip(block_cols[0, 0] - out_place * tile_cols, 0, tile_cols - 1)
    live = jnp.arange(MAXB, dtype=jnp.int32) < counts[0, 0]
    mine_half = (local_rows // half_rows) == core
    use_mine = (live & mine_half).astype(jnp.int32)
    use_other = (live & ~mine_half).astype(jnp.int32)
    in_half = (local_rows % half_rows).astype(jnp.int32)
    place = jnp.stack([z_me, y_me]).astype(jnp.int32)

    width = half_rows * BLK
    first, second = activations[:, :width], activations[:, width:]
    on_first = core == 0
    keep = jnp.where(on_first, first, second)
    send = jnp.where(on_first, second, first)
    swap = [(0, 1), (1, 0)]
    recv = lax.ppermute(send, "core", swap)
    lead = jnp.where(on_first, keep, recv)
    trail = jnp.where(on_first, recv, keep)

    lead_z = jnp.stack(relative_gather(lead, "z", nz), 0)
    lead_all = jnp.stack(relative_gather(lead_z, "y", ny), 1)
    trail_y = jnp.stack(relative_gather(trail, "y", ny), 0)
    trail_all = jnp.stack(relative_gather(trail_y, "z", nz), 0)
    lead_all = lead_all.reshape(nz * ny, tok, width)
    trail_all = trail_all.reshape(nz * ny, tok, width)

    grad_pieces, starts = ring_gather(out_grad, "in", in_place)
    lead_all, trail_all, grad_pieces = lax.optimization_barrier((lead_all, trail_all, grad_pieces))
    grad_pieces = [g.reshape(g.shape[0] // (2 * tok), 2, tok, g.shape[1]) for g in grad_pieces]
    starts = starts // (2 * tok)
    lead_other = lax.ppermute(lead_all, "core", swap)
    trail_other = lax.ppermute(trail_all, "core", swap)
    part_mine = block_products(
        lead_all, trail_all, grad_pieces, starts, place, in_half, local_cols, use_mine, ny
    )
    part_other = block_products(
        lead_other, trail_other, grad_pieces, starts, place, in_half, local_cols, use_other, ny
    )
    totals = part_mine + part_other
    return totals.reshape(1, 1, MAXB, BLK, BLK)


def solution(mesh):
    n_in, n_out = mesh.devices.shape
    row = mesh.devices[0]
    ny = len({d.coords[1] for d in row})
    ncore = n_out // len({tuple(d.coords) for d in row})
    nz = n_out // (ny * ncore)
    split = jax.sharding.Mesh(
        mesh.devices.reshape(n_in, nz, ny, ncore), ("in", "z", "y", "core")
    )
    out = ("z", "y", "core")
    return jax.shard_map(
        on_device,
        mesh=split,
        in_specs=(
            P(out, "in"),
            P("in", out),
            P("in", out, None),
            P("in", out, None),
            P("in", out),
        ),
        out_specs=P("in", out, None, None, None),
        check_vma=False,
    )
```

```python
import functools

import jax
import jax.numpy as jnp
from jax import lax
from jax.experimental import pallas as pl
from jax.experimental.pallas import tpu as pltpu
from jax.sharding import PartitionSpec as P

BLK = 128
MAXB = 4


def block_kernel(n_grad, ny, rows_ref, cols_ref, use_ref, starts_ref, place_ref, *rest):
    first_hbm, second_hbm = rest[0], rest[1]
    grad_hbm = rest[2:2 + n_grad]
    out_ref, a_v, g_v, sems = rest[2 + n_grad:]
    chunks = a_v.shape[2]

    copies = []
    for s in range(MAXB):
        r = pl.multiple_of(rows_ref[s] * BLK, BLK)
        c = pl.multiple_of(cols_ref[s] * BLK, BLK)
        slot = [
            pltpu.make_async_copy(first_hbm.at[:, :, pl.ds(r, BLK)], a_v.at[s, 0], sems.at[s, 0]),
            pltpu.make_async_copy(second_hbm.at[:, :, pl.ds(r, BLK)], a_v.at[s, 1], sems.at[s, 1]),
        ]
        for p, piece in enumerate(grad_hbm):
            slot.append(
                pltpu.make_async_copy(
                    piece.at[:, :, :, pl.ds(c, BLK)],
                    g_v.at[s, pl.ds(starts_ref[p], piece.shape[0])],
                    sems.at[s, p + 2],
                )
            )

        @pl.when(use_ref[s] == 1)
        def _(slot=slot):
            for cp in slot:
                cp.start()

        copies.append(slot)

    z_me, y_me = place_ref[0], place_ref[1]
    nz = chunks // ny
    for s in range(MAXB):

        @pl.when(use_ref[s] == 0)
        def _(s=s):
            out_ref[s] = jnp.zeros((BLK, BLK), jnp.float32)

        @pl.when(use_ref[s] == 1)
        def _(s=s):
            for cp in copies[s]:
                cp.wait()

            def body(k, acc):
                pair = ((z_me + k // ny) % nz) * ny + (y_me + k % ny) % ny
                for half in range(2):
                    a = a_v[s, half, k]
                    g = g_v[s, pair, half]
                    acc = acc + lax.dot_general(
                        a, g, (((0,), (0,)), ((), ())), preferred_element_type=jnp.float32
                    )
                return acc

            out_ref[s] = lax.fori_loop(0, chunks, body, jnp.zeros((BLK, BLK), jnp.float32))


def block_products(first, second, grad_pieces, starts, place, local_rows, local_cols, use, ny):
    chunks, tok, width = first.shape
    n_grad = len(grad_pieces)
    smem = pl.BlockSpec(memory_space=pltpu.SMEM)
    hbm = pl.BlockSpec(memory_space=pl.ANY)
    tokens = 2 * chunks * tok
    flops = 2 * MAXB * tokens * BLK * BLK
    moved = 2 * MAXB * tokens * BLK * 2 + MAXB * BLK * BLK * 4
    return pl.pallas_call(
        functools.partial(block_kernel, n_grad, ny),
        out_shape=jax.ShapeDtypeStruct((MAXB, BLK, BLK), jnp.float32),
        in_specs=[smem] * 5 + [hbm] * (2 + n_grad),
        out_specs=pl.BlockSpec(memory_space=pltpu.VMEM),
        scratch_shapes=[
            pltpu.VMEM((MAXB, 2, chunks, tok, BLK), jnp.bfloat16),
            pltpu.VMEM((MAXB, chunks, 2, tok, BLK), jnp.bfloat16),
            pltpu.SemaphoreType.DMA((MAXB, 2 + n_grad)),
        ],
        compiler_params=pltpu.CompilerParams(vmem_limit_bytes=48 * 1024 * 1024),
        cost_estimate=pl.CostEstimate(flops=flops, bytes_accessed=moved, transcendentals=0),
    )(local_rows, local_cols, use, starts, place, first, second, *grad_pieces)


def relative_gather(x, axis, n):
    right = [(k, (k + 1) % n) for k in range(n)]
    left = [(k, (k - 1) % n) for k in range(n)]
    rel = [x] + [None] * (n - 1)
    from_left, from_right = x, x
    for t in range(1, (n + 1) // 2):
        from_left = lax.ppermute(from_left, axis, right)
        from_right = lax.ppermute(from_right, axis, left)
        rel[n - t] = from_left
        rel[t] = from_right
    if n % 2 == 0 and n > 1:
        t = n // 2
        half = x.shape[0] // 2
        near_a = lax.ppermute(from_left[:half], axis, right)
        near_b = lax.ppermute(from_right[half:], axis, left)
        rel[t] = jnp.concatenate([near_a, near_b], 0)
    return rel


def ring_gather(own, axis, place):
    n = lax.axis_size(axis)
    length = own.shape[0]
    right = [(k, (k + 1) % n) for k in range(n)]
    left = [(k, (k - 1) % n) for k in range(n)]
    pieces, starts = [own], [place * length]
    from_left, from_right = own, own
    for d in range(1, (n + 1) // 2):
        from_left = lax.ppermute(from_left, axis, right)
        from_right = lax.ppermute(from_right, axis, left)
        pieces += [from_left, from_right]
        starts += [((place - d) % n) * length, ((place + d) % n) * length]
    if n % 2 == 0 and n > 1:
        half = length // 2
        d = n // 2
        if d == 1:
            near_a, near_b = lax.ppermute(own[:half], axis, right), lax.ppermute(own[half:], axis, left)
        else:
            near_a = lax.ppermute(from_left[:half], axis, right)
            near_b = lax.ppermute(from_right[half:], axis, left)
        far = ((place + d) % n) * length
        pieces += [near_a, near_b]
        starts += [far, far + half]
    return pieces, jnp.stack(starts).astype(jnp.int32)


def on_device(activations, out_grad, block_rows, block_cols, counts):
    in_place = lax.axis_index("in")
    core = lax.axis_index("core")
    nz, ny, ncore = lax.axis_size("z"), lax.axis_size("y"), lax.axis_size("core")
    z_me, y_me = lax.axis_index("z"), lax.axis_index("y")
    out_place = (z_me * ny + y_me) * ncore + core
    tok = activations.shape[0]
    tile_rows = activations.shape[1] // BLK
    tile_cols = out_grad.shape[1] // BLK
    half_rows = tile_rows // 2
    local_rows = jnp.clip(block_rows[0, 0] - in_place * tile_rows, 0, tile_rows - 1)
    local_cols = jnp.clip(block_cols[0, 0] - out_place * tile_cols, 0, tile_cols - 1)
    live = jnp.arange(MAXB, dtype=jnp.int32) < counts[0, 0]
    mine_half = (local_rows // half_rows) == core
    use_mine = (live & mine_half).astype(jnp.int32)
    use_other = (live & ~mine_half).astype(jnp.int32)
    in_half = (local_rows % half_rows).astype(jnp.int32)
    place = jnp.stack([z_me, y_me]).astype(jnp.int32)

    width = half_rows * BLK
    first, second = activations[:, :width], activations[:, width:]
    on_first = core == 0
    keep = jnp.where(on_first, first, second)
    send = jnp.where(on_first, second, first)
    swap = [(0, 1), (1, 0)]
    recv = lax.ppermute(send, "core", swap)
    lead = jnp.where(on_first, keep, recv)
    trail = jnp.where(on_first, recv, keep)

    lead_z = jnp.stack(relative_gather(lead, "z", nz), 0)
    lead_all = jnp.stack(relative_gather(lead_z, "y", ny), 1)
    trail_y = jnp.stack(relative_gather(trail, "y", ny), 0)
    trail_all = jnp.stack(relative_gather(trail_y, "z", nz), 0)
    lead_all = lead_all.reshape(nz * ny, tok, width)
    trail_all = trail_all.reshape(nz * ny, tok, width)

    grad_pieces = [lax.all_gather(out_grad, "in", axis=0, tiled=True)]
    starts = jnp.zeros((1,), jnp.int32)
    lead_all, trail_all, grad_pieces = lax.optimization_barrier((lead_all, trail_all, grad_pieces))
    grad_pieces = [g.reshape(g.shape[0] // (2 * tok), 2, tok, g.shape[1]) for g in grad_pieces]
    starts = starts // (2 * tok)
    lead_other = lax.ppermute(lead_all, "core", swap)
    trail_other = lax.ppermute(trail_all, "core", swap)
    part_mine = block_products(
        lead_all, trail_all, grad_pieces, starts, place, in_half, local_cols, use_mine, ny
    )
    part_other = block_products(
        lead_other, trail_other, grad_pieces, starts, place, in_half, local_cols, use_other, ny
    )
    totals = part_mine + part_other
    return totals.reshape(1, 1, MAXB, BLK, BLK)


def solution(mesh):
    n_in, n_out = mesh.devices.shape
    row = mesh.devices[0]
    ny = len({d.coords[1] for d in row})
    ncore = n_out // len({tuple(d.coords) for d in row})
    nz = n_out // (ny * ncore)
    split = jax.sharding.Mesh(
        mesh.devices.reshape(n_in, nz, ny, ncore), ("in", "z", "y", "core")
    )
    out = ("z", "y", "core")
    return jax.shard_map(
        on_device,
        mesh=split,
        in_specs=(
            P(out, "in"),
            P("in", out),
            P("in", out, None),
            P("in", out, None),
            P("in", out),
        ),
        out_specs=P("in", out, None, None, None),
        check_vma=False,
    )
```

```python
import functools

import jax
import jax.numpy as jnp
from jax import lax
from jax.experimental import pallas as pl
from jax.experimental.pallas import tpu as pltpu
from jax.sharding import PartitionSpec as P

BLK = 128
MAXB = 4


def block_kernel(n_grad, ny, rows_ref, cols_ref, use_ref, starts_ref, place_ref, *rest):
    first_hbm, second_hbm = rest[0], rest[1]
    grad_hbm = rest[2:2 + n_grad]
    out_ref, a_v, g_v, sems = rest[2 + n_grad:]
    chunks, _, tok, _ = a_v.shape[1:]

    copies = []
    for s in range(MAXB):
        r = pl.multiple_of(rows_ref[s] * BLK, BLK)
        c = pl.multiple_of(cols_ref[s] * BLK, BLK)
        slot = [
            pltpu.make_async_copy(first_hbm.at[:, :, pl.ds(r, BLK)], a_v.at[s, :, 0], sems.at[s, 0]),
            pltpu.make_async_copy(second_hbm.at[:, :, pl.ds(r, BLK)], a_v.at[s, :, 1], sems.at[s, 1]),
        ]
        for p, piece in enumerate(grad_hbm):
            slot.append(
                pltpu.make_async_copy(
                    piece.at[:, :, :, pl.ds(c, BLK)],
                    g_v.at[s, pl.ds(starts_ref[p], piece.shape[0])],
                    sems.at[s, p + 2],
                )
            )

        @pl.when(use_ref[s] == 1)
        def _(slot=slot):
            for cp in slot:
                cp.start()

        copies.append(slot)

    z_me, y_me = place_ref[0], place_ref[1]
    nz = chunks // ny
    for s in range(MAXB):

        @pl.when(use_ref[s] == 0)
        def _(s=s):
            out_ref[s] = jnp.zeros((BLK, BLK), jnp.float32)

        @pl.when(use_ref[s] == 1)
        def _(s=s):
            for cp in copies[s]:
                cp.wait()

            def body(k, acc):
                pair = ((z_me + k // ny) % nz) * ny + (y_me + k % ny) % ny
                a = a_v[s, k].reshape(2 * tok, BLK)
                g = g_v[s, pair].reshape(2 * tok, BLK)
                return acc + lax.dot_general(
                    a, g, (((0,), (0,)), ((), ())), preferred_element_type=jnp.float32
                )

            out_ref[s] = lax.fori_loop(
                0, chunks, body, jnp.zeros((BLK, BLK), jnp.float32), unroll=2
            )


def block_products(first, second, grad_pieces, starts, place, local_rows, local_cols, use, ny):
    chunks, tok, width = first.shape
    n_grad = len(grad_pieces)
    smem = pl.BlockSpec(memory_space=pltpu.SMEM)
    hbm = pl.BlockSpec(memory_space=pl.ANY)
    tokens = 2 * chunks * tok
    flops = 2 * MAXB * tokens * BLK * BLK
    moved = 2 * MAXB * tokens * BLK * 2 + MAXB * BLK * BLK * 4
    return pl.pallas_call(
        functools.partial(block_kernel, n_grad, ny),
        out_shape=jax.ShapeDtypeStruct((MAXB, BLK, BLK), jnp.float32),
        in_specs=[smem] * 5 + [hbm] * (2 + n_grad),
        out_specs=pl.BlockSpec(memory_space=pltpu.VMEM),
        scratch_shapes=[
            pltpu.VMEM((MAXB, chunks, 2, tok, BLK), jnp.bfloat16),
            pltpu.VMEM((MAXB, chunks, 2, tok, BLK), jnp.bfloat16),
            pltpu.SemaphoreType.DMA((MAXB, 2 + n_grad)),
        ],
        compiler_params=pltpu.CompilerParams(vmem_limit_bytes=48 * 1024 * 1024),
        cost_estimate=pl.CostEstimate(flops=flops, bytes_accessed=moved, transcendentals=0),
    )(local_rows, local_cols, use, starts, place, first, second, *grad_pieces)


def relative_gather(x, axis, n):
    right = [(k, (k + 1) % n) for k in range(n)]
    left = [(k, (k - 1) % n) for k in range(n)]
    rel = [x] + [None] * (n - 1)
    from_left, from_right = x, x
    for t in range(1, (n + 1) // 2):
        from_left = lax.ppermute(from_left, axis, right)
        from_right = lax.ppermute(from_right, axis, left)
        rel[n - t] = from_left
        rel[t] = from_right
    if n % 2 == 0 and n > 1:
        t = n // 2
        half = x.shape[0] // 2
        near_a = lax.ppermute(from_left[:half], axis, right)
        near_b = lax.ppermute(from_right[half:], axis, left)
        rel[t] = jnp.concatenate([near_a, near_b], 0)
    return rel


def ring_gather(own, axis, place):
    n = lax.axis_size(axis)
    length = own.shape[0]
    right = [(k, (k + 1) % n) for k in range(n)]
    left = [(k, (k - 1) % n) for k in range(n)]
    pieces, starts = [own], [place * length]
    from_left, from_right = own, own
    for d in range(1, (n + 1) // 2):
        from_left = lax.ppermute(from_left, axis, right)
        from_right = lax.ppermute(from_right, axis, left)
        pieces += [from_left, from_right]
        starts += [((place - d) % n) * length, ((place + d) % n) * length]
    if n % 2 == 0 and n > 1:
        half = length // 2
        d = n // 2
        if d == 1:
            near_a, near_b = lax.ppermute(own[:half], axis, right), lax.ppermute(own[half:], axis, left)
        else:
            near_a = lax.ppermute(from_left[:half], axis, right)
            near_b = lax.ppermute(from_right[half:], axis, left)
        far = ((place + d) % n) * length
        pieces += [near_a, near_b]
        starts += [far, far + half]
    return pieces, jnp.stack(starts).astype(jnp.int32)


def on_device(activations, out_grad, block_rows, block_cols, counts):
    in_place = lax.axis_index("in")
    core = lax.axis_index("core")
    nz, ny, ncore = lax.axis_size("z"), lax.axis_size("y"), lax.axis_size("core")
    z_me, y_me = lax.axis_index("z"), lax.axis_index("y")
    out_place = (z_me * ny + y_me) * ncore + core
    tok = activations.shape[0]
    tile_rows = activations.shape[1] // BLK
    tile_cols = out_grad.shape[1] // BLK
    half_rows = tile_rows // 2
    local_rows = jnp.clip(block_rows[0, 0] - in_place * tile_rows, 0, tile_rows - 1)
    local_cols = jnp.clip(block_cols[0, 0] - out_place * tile_cols, 0, tile_cols - 1)
    live = jnp.arange(MAXB, dtype=jnp.int32) < counts[0, 0]
    mine_half = (local_rows // half_rows) == core
    use_mine = (live & mine_half).astype(jnp.int32)
    use_other = (live & ~mine_half).astype(jnp.int32)
    in_half = (local_rows % half_rows).astype(jnp.int32)
    place = jnp.stack([z_me, y_me]).astype(jnp.int32)

    width = half_rows * BLK
    first, second = activations[:, :width], activations[:, width:]
    on_first = core == 0
    keep = jnp.where(on_first, first, second)
    send = jnp.where(on_first, second, first)
    swap = [(0, 1), (1, 0)]
    recv = lax.ppermute(send, "core", swap)
    lead = jnp.where(on_first, keep, recv)
    trail = jnp.where(on_first, recv, keep)

    lead_z = jnp.stack(relative_gather(lead, "z", nz), 0)
    lead_all = jnp.stack(relative_gather(lead_z, "y", ny), 1)
    trail_y = jnp.stack(relative_gather(trail, "y", ny), 0)
    trail_all = jnp.stack(relative_gather(trail_y, "z", nz), 0)
    lead_all = lead_all.reshape(nz * ny, tok, width)
    trail_all = trail_all.reshape(nz * ny, tok, width)

    grad_pieces, starts = ring_gather(out_grad, "in", in_place)
    lead_all, trail_all, grad_pieces = lax.optimization_barrier((lead_all, trail_all, grad_pieces))
    grad_pieces = [g.reshape(g.shape[0] // (2 * tok), 2, tok, g.shape[1]) for g in grad_pieces]
    starts = starts // (2 * tok)
    lead_other = lax.ppermute(lead_all, "core", swap)
    trail_other = lax.ppermute(trail_all, "core", swap)
    part_mine = block_products(
        lead_all, trail_all, grad_pieces, starts, place, in_half, local_cols, use_mine, ny
    )
    part_other = block_products(
        lead_other, trail_other, grad_pieces, starts, place, in_half, local_cols, use_other, ny
    )
    totals = part_mine + part_other
    return totals.reshape(1, 1, MAXB, BLK, BLK)


def solution(mesh):
    n_in, n_out = mesh.devices.shape
    row = mesh.devices[0]
    ny = len({d.coords[1] for d in row})
    ncore = n_out // len({tuple(d.coords) for d in row})
    nz = n_out // (ny * ncore)
    split = jax.sharding.Mesh(
        mesh.devices.reshape(n_in, nz, ny, ncore), ("in", "z", "y", "core")
    )
    out = ("z", "y", "core")
    return jax.shard_map(
        on_device,
        mesh=split,
        in_specs=(
            P(out, "in"),
            P("in", out),
            P("in", out, None),
            P("in", out, None),
            P("in", out),
        ),
        out_specs=P("in", out, None, None, None),
        check_vma=False,
    )
```

```python
import functools

import jax
import jax.numpy as jnp
from jax import lax
from jax.experimental import pallas as pl
from jax.experimental.pallas import tpu as pltpu
from jax.sharding import PartitionSpec as P

BLK = 128
MAXB = 4
GROUP = 4


def block_kernel(n_grad, ny, rows_ref, cols_ref, use_ref, starts_ref, place_ref, *rest):
    first_hbm, second_hbm = rest[0], rest[1]
    grad_hbm = rest[2:2 + n_grad]
    out_ref, a_v, g_v, act_sems, grad_sems = rest[2 + n_grad:]
    chunks = a_v.shape[0]
    nz = chunks // ny
    z_me, y_me = place_ref[0], place_ref[1]
    any_use = use_ref[0] + use_ref[1] + use_ref[2] + use_ref[3] > 0

    act_copies = []
    for s in range(MAXB):
        r = pl.multiple_of(rows_ref[s] * BLK, BLK)
        lanes = pl.ds(s * BLK, BLK)
        slot = [
            pltpu.make_async_copy(
                first_hbm.at[:, :, pl.ds(r, BLK)], a_v.at[:, 0, :, lanes], act_sems.at[s, 0]
            ),
            pltpu.make_async_copy(
                second_hbm.at[:, :, pl.ds(r, BLK)], a_v.at[:, 1, :, lanes], act_sems.at[s, 1]
            ),
        ]

        @pl.when(use_ref[s] == 1)
        def _(slot=slot):
            for cp in slot:
                cp.start()

        act_copies.append(slot)

    grad_copies = []
    for p, piece in enumerate(grad_hbm):
        for j in range(piece.shape[0]):
            q = starts_ref[p] + j
            k = ((q // ny - z_me + nz) % nz) * ny + (q % ny - y_me + ny) % ny
            grad_copies.append(
                pltpu.make_async_copy(piece.at[j], g_v.at[k], grad_sems.at[len(grad_copies)])
            )

    @pl.when(any_use)
    def _():
        for cp in grad_copies:
            cp.start()

    for s in range(MAXB):

        @pl.when(use_ref[s] == 1)
        def _(s=s):
            for cp in act_copies[s]:
                cp.wait()

    @pl.when(jnp.logical_not(any_use))
    def _():
        out_ref[...] = jnp.zeros(out_ref.shape, jnp.float32)

    @pl.when(any_use)
    def _():
        for cp in grad_copies:
            cp.wait()
        step = GROUP
        rows = step * a_v.shape[1] * a_v.shape[2]

        def body(kb, acc):
            k0 = pl.multiple_of(kb * step, step)
            a = a_v[pl.ds(k0, step)].reshape(rows, a_v.shape[3])
            g = g_v[pl.ds(k0, step)].reshape(rows, g_v.shape[3])
            return acc + lax.dot_general(
                a, g, (((0,), (0,)), ((), ())), preferred_element_type=jnp.float32
            )

        acc = lax.fori_loop(
            0, chunks // step, body, jnp.zeros((a_v.shape[3], g_v.shape[3]), jnp.float32)
        )
        for s in range(MAXB):
            blk = acc[s * BLK:(s + 1) * BLK]
            pick = jnp.where(cols_ref[s] == 0, blk[:, :BLK], blk[:, BLK:2 * BLK])
            out_ref[s] = jnp.where(use_ref[s] == 1, pick, jnp.zeros_like(pick))


def block_products(first, second, grad_pieces, starts, place, local_rows, local_cols, use, ny):
    chunks, tok, width = first.shape
    n_grad = len(grad_pieces)
    n_pairs = sum(g.shape[0] for g in grad_pieces)
    cols = grad_pieces[0].shape[3]
    smem = pl.BlockSpec(memory_space=pltpu.SMEM)
    hbm = pl.BlockSpec(memory_space=pl.ANY)
    tokens = 2 * chunks * tok
    flops = 2 * tokens * MAXB * BLK * cols
    moved = MAXB * tokens * BLK * 2 + tokens * cols * 2 + MAXB * BLK * BLK * 4
    return pl.pallas_call(
        functools.partial(block_kernel, n_grad, ny),
        out_shape=jax.ShapeDtypeStruct((MAXB, BLK, BLK), jnp.float32),
        in_specs=[smem] * 5 + [hbm] * (2 + n_grad),
        out_specs=pl.BlockSpec(memory_space=pltpu.VMEM),
        scratch_shapes=[
            pltpu.VMEM((chunks, 2, tok, MAXB * BLK), jnp.bfloat16),
            pltpu.VMEM((chunks, 2, tok, cols), jnp.bfloat16),
            pltpu.SemaphoreType.DMA((MAXB, 2)),
            pltpu.SemaphoreType.DMA((n_pairs,)),
        ],
        compiler_params=pltpu.CompilerParams(vmem_limit_bytes=48 * 1024 * 1024),
        cost_estimate=pl.CostEstimate(flops=flops, bytes_accessed=moved, transcendentals=0),
    )(local_rows, local_cols, use, starts, place, first, second, *grad_pieces)


def relative_gather(x, axis, n):
    right = [(k, (k + 1) % n) for k in range(n)]
    left = [(k, (k - 1) % n) for k in range(n)]
    rel = [x] + [None] * (n - 1)
    from_left, from_right = x, x
    for t in range(1, (n + 1) // 2):
        from_left = lax.ppermute(from_left, axis, right)
        from_right = lax.ppermute(from_right, axis, left)
        rel[n - t] = from_left
        rel[t] = from_right
    if n % 2 == 0 and n > 1:
        t = n // 2
        half = x.shape[0] // 2
        near_a = lax.ppermute(from_left[:half], axis, right)
        near_b = lax.ppermute(from_right[half:], axis, left)
        rel[t] = jnp.concatenate([near_a, near_b], 0)
    return rel


def ring_gather(own, axis, place):
    n = lax.axis_size(axis)
    length = own.shape[0]
    right = [(k, (k + 1) % n) for k in range(n)]
    left = [(k, (k - 1) % n) for k in range(n)]
    pieces, starts = [own], [place * length]
    from_left, from_right = own, own
    for d in range(1, (n + 1) // 2):
        from_left = lax.ppermute(from_left, axis, right)
        from_right = lax.ppermute(from_right, axis, left)
        pieces += [from_left, from_right]
        starts += [((place - d) % n) * length, ((place + d) % n) * length]
    if n % 2 == 0 and n > 1:
        half = length // 2
        d = n // 2
        if d == 1:
            near_a, near_b = lax.ppermute(own[:half], axis, right), lax.ppermute(own[half:], axis, left)
        else:
            near_a = lax.ppermute(from_left[:half], axis, right)
            near_b = lax.ppermute(from_right[half:], axis, left)
        far = ((place + d) % n) * length
        pieces += [near_a, near_b]
        starts += [far, far + half]
    return pieces, jnp.stack(starts).astype(jnp.int32)


def on_device(activations, out_grad, block_rows, block_cols, counts):
    in_place = lax.axis_index("in")
    core = lax.axis_index("core")
    nz, ny, ncore = lax.axis_size("z"), lax.axis_size("y"), lax.axis_size("core")
    z_me, y_me = lax.axis_index("z"), lax.axis_index("y")
    out_place = (z_me * ny + y_me) * ncore + core
    tok = activations.shape[0]
    tile_rows = activations.shape[1] // BLK
    tile_cols = out_grad.shape[1] // BLK
    half_rows = tile_rows // 2
    local_rows = jnp.clip(block_rows[0, 0] - in_place * tile_rows, 0, tile_rows - 1)
    local_cols = jnp.clip(block_cols[0, 0] - out_place * tile_cols, 0, tile_cols - 1)
    live = jnp.arange(MAXB, dtype=jnp.int32) < counts[0, 0]
    mine_half = (local_rows // half_rows) == core
    use_mine = (live & mine_half).astype(jnp.int32)
    use_other = (live & ~mine_half).astype(jnp.int32)
    in_half = (local_rows % half_rows).astype(jnp.int32)
    place = jnp.stack([z_me, y_me]).astype(jnp.int32)

    width = half_rows * BLK
    first, second = activations[:, :width], activations[:, width:]
    on_first = core == 0
    keep = jnp.where(on_first, first, second)
    send = jnp.where(on_first, second, first)
    swap = [(0, 1), (1, 0)]
    recv = lax.ppermute(send, "core", swap)
    lead = jnp.where(on_first, keep, recv)
    trail = jnp.where(on_first, recv, keep)

    lead_z = jnp.stack(relative_gather(lead, "z", nz), 0)
    lead_all = jnp.stack(relative_gather(lead_z, "y", ny), 1)
    trail_y = jnp.stack(relative_gather(trail, "y", ny), 0)
    trail_all = jnp.stack(relative_gather(trail_y, "z", nz), 0)
    lead_all = lead_all.reshape(nz * ny, tok, width)
    trail_all = trail_all.reshape(nz * ny, tok, width)

    grad_pieces, starts = ring_gather(out_grad, "in", in_place)
    lead_all, trail_all, grad_pieces = lax.optimization_barrier((lead_all, trail_all, grad_pieces))
    grad_pieces = [g.reshape(g.shape[0] // (2 * tok), 2, tok, g.shape[1]) for g in grad_pieces]
    starts = starts // (2 * tok)
    lead_other = lax.ppermute(lead_all, "core", swap)
    trail_other = lax.ppermute(trail_all, "core", swap)
    part_mine = block_products(
        lead_all, trail_all, grad_pieces, starts, place, in_half, local_cols, use_mine, ny
    )
    part_other = block_products(
        lead_other, trail_other, grad_pieces, starts, place, in_half, local_cols, use_other, ny
    )
    totals = part_mine + part_other
    return totals.reshape(1, 1, MAXB, BLK, BLK)


def solution(mesh):
    n_in, n_out = mesh.devices.shape
    row = mesh.devices[0]
    ny = len({d.coords[1] for d in row})
    ncore = n_out // len({tuple(d.coords) for d in row})
    nz = n_out // (ny * ncore)
    split = jax.sharding.Mesh(
        mesh.devices.reshape(n_in, nz, ny, ncore), ("in", "z", "y", "core")
    )
    out = ("z", "y", "core")
    return jax.shard_map(
        on_device,
        mesh=split,
        in_specs=(
            P(out, "in"),
            P("in", out),
            P("in", out, None),
            P("in", out, None),
            P("in", out),
        ),
        out_specs=P("in", out, None, None, None),
        check_vma=False,
    )
```

```python
import functools

import jax
import jax.numpy as jnp
from jax import lax
from jax.experimental import pallas as pl
from jax.experimental.pallas import tpu as pltpu
from jax.sharding import PartitionSpec as P

BLK = 128
MAXB = 4


def block_kernel(n_grad, ny, rows_ref, cols_ref, use_ref, starts_ref, place_ref, *rest):
    first_hbm, second_hbm = rest[0], rest[1]
    grad_hbm = rest[2:2 + n_grad]
    out_ref, a_v, g_v, sems = rest[2 + n_grad:]
    chunks, _, tok, _ = a_v.shape[1:]

    copies = []
    for s in range(MAXB):
        r = pl.multiple_of(rows_ref[s] * BLK, BLK)
        c = pl.multiple_of(cols_ref[s] * BLK, BLK)
        slot = [
            pltpu.make_async_copy(first_hbm.at[:, :, pl.ds(r, BLK)], a_v.at[s, :, 0], sems.at[s, 0]),
            pltpu.make_async_copy(second_hbm.at[:, :, pl.ds(r, BLK)], a_v.at[s, :, 1], sems.at[s, 1]),
        ]
        for p, piece in enumerate(grad_hbm):
            slot.append(
                pltpu.make_async_copy(
                    piece.at[:, :, :, pl.ds(c, BLK)],
                    g_v.at[s, pl.ds(starts_ref[p], piece.shape[0])],
                    sems.at[s, p + 2],
                )
            )

        @pl.when(use_ref[s] == 1)
        def _(slot=slot):
            for cp in slot:
                cp.start()

        copies.append(slot)

    z_me, y_me = place_ref[0], place_ref[1]
    nz = chunks // ny
    for s in range(MAXB):

        @pl.when(use_ref[s] == 0)
        def _(s=s):
            out_ref[s] = jnp.zeros((BLK, BLK), jnp.float32)

        @pl.when(use_ref[s] == 1)
        def _(s=s):
            for cp in copies[s]:
                cp.wait()

            def body(k, acc):
                pair = ((z_me + k // ny) % nz) * ny + (y_me + k % ny) % ny
                a = a_v[s, k].reshape(2 * tok, BLK)
                g = g_v[s, pair].reshape(2 * tok, BLK)
                return acc + lax.dot_general(
                    a, g, (((0,), (0,)), ((), ())), preferred_element_type=jnp.float32
                )

            out_ref[s] = lax.fori_loop(
                0, chunks, body, jnp.zeros((BLK, BLK), jnp.float32), unroll=2
            )


def block_products(first, second, grad_pieces, starts, place, local_rows, local_cols, use, ny):
    chunks, tok, width = first.shape
    n_grad = len(grad_pieces)
    smem = pl.BlockSpec(memory_space=pltpu.SMEM)
    hbm = pl.BlockSpec(memory_space=pl.ANY)
    tokens = 2 * chunks * tok
    flops = 2 * MAXB * tokens * BLK * BLK
    moved = 2 * MAXB * tokens * BLK * 2 + MAXB * BLK * BLK * 4
    return pl.pallas_call(
        functools.partial(block_kernel, n_grad, ny),
        out_shape=jax.ShapeDtypeStruct((MAXB, BLK, BLK), jnp.float32),
        in_specs=[smem] * 5 + [hbm] * (2 + n_grad),
        out_specs=pl.BlockSpec(memory_space=pltpu.VMEM),
        scratch_shapes=[
            pltpu.VMEM((MAXB, chunks, 2, tok, BLK), jnp.bfloat16),
            pltpu.VMEM((MAXB, chunks, 2, tok, BLK), jnp.bfloat16),
            pltpu.SemaphoreType.DMA((MAXB, 2 + n_grad)),
        ],
        compiler_params=pltpu.CompilerParams(vmem_limit_bytes=48 * 1024 * 1024),
        cost_estimate=pl.CostEstimate(flops=flops, bytes_accessed=moved, transcendentals=0),
    )(local_rows, local_cols, use, starts, place, first, second, *grad_pieces)


def relative_gather(x, axis, n):
    right = [(k, (k + 1) % n) for k in range(n)]
    left = [(k, (k - 1) % n) for k in range(n)]
    rel = [x] + [None] * (n - 1)
    from_left, from_right = x, x
    for t in range(1, (n + 1) // 2):
        from_left = lax.ppermute(from_left, axis, right)
        from_right = lax.ppermute(from_right, axis, left)
        rel[n - t] = from_left
        rel[t] = from_right
    if n % 2 == 0 and n > 1:
        t = n // 2
        half = x.shape[0] // 2
        near_a = lax.ppermute(from_left[:half], axis, right)
        near_b = lax.ppermute(from_right[half:], axis, left)
        rel[t] = jnp.concatenate([near_a, near_b], 0)
    return rel


def ring_gather(own, axis, place):
    n = lax.axis_size(axis)
    length = own.shape[0]
    right = [(k, (k + 1) % n) for k in range(n)]
    left = [(k, (k - 1) % n) for k in range(n)]
    pieces, starts = [own], [place * length]
    from_left, from_right = own, own
    for d in range(1, (n + 1) // 2):
        from_left = lax.ppermute(from_left, axis, right)
        from_right = lax.ppermute(from_right, axis, left)
        pieces += [from_left, from_right]
        starts += [((place - d) % n) * length, ((place + d) % n) * length]
    if n % 2 == 0 and n > 1:
        half = length // 2
        d = n // 2
        if d == 1:
            near_a, near_b = lax.ppermute(own[:half], axis, right), lax.ppermute(own[half:], axis, left)
        else:
            near_a = lax.ppermute(from_left[:half], axis, right)
            near_b = lax.ppermute(from_right[half:], axis, left)
        far = ((place + d) % n) * length
        pieces += [near_a, near_b]
        starts += [far, far + half]
    return pieces, jnp.stack(starts).astype(jnp.int32)


def on_device(activations, out_grad, block_rows, block_cols, counts):
    in_place = lax.axis_index("in")
    core = lax.axis_index("core")
    nz, ny, ncore = lax.axis_size("z"), lax.axis_size("y"), lax.axis_size("core")
    z_me, y_me = lax.axis_index("z"), lax.axis_index("y")
    out_place = (z_me * ny + y_me) * ncore + core
    tok = activations.shape[0]
    tile_rows = activations.shape[1] // BLK
    tile_cols = out_grad.shape[1] // BLK
    half_rows = tile_rows // 2
    local_rows = jnp.clip(block_rows[0, 0] - in_place * tile_rows, 0, tile_rows - 1)
    local_cols = jnp.clip(block_cols[0, 0] - out_place * tile_cols, 0, tile_cols - 1)
    live = jnp.arange(MAXB, dtype=jnp.int32) < counts[0, 0]
    mine_half = (local_rows // half_rows) == core
    use_mine = (live & mine_half).astype(jnp.int32)
    use_other = (live & ~mine_half).astype(jnp.int32)
    in_half = (local_rows % half_rows).astype(jnp.int32)
    place = jnp.stack([jnp.zeros_like(z_me), y_me]).astype(jnp.int32)

    width = half_rows * BLK
    first, second = activations[:, :width], activations[:, width:]
    on_first = core == 0
    keep = jnp.where(on_first, first, second)
    send = jnp.where(on_first, second, first)
    swap = [(0, 1), (1, 0)]
    recv = lax.ppermute(send, "core", swap)
    lead = jnp.where(on_first, keep, recv)
    trail = jnp.where(on_first, recv, keep)

    lead_z = lax.all_gather(lead, "z", axis=0)
    lead_all = jnp.stack(relative_gather(lead_z, "y", ny), 1)
    trail_y = jnp.stack(relative_gather(trail, "y", ny), 0)
    trail_all = lax.all_gather(trail_y, "z", axis=0)
    lead_all = lead_all.reshape(nz * ny, tok, width)
    trail_all = trail_all.reshape(nz * ny, tok, width)

    grad_pieces, starts = ring_gather(out_grad, "in", in_place)
    lead_all, trail_all, grad_pieces = lax.optimization_barrier((lead_all, trail_all, grad_pieces))
    grad_pieces = [g.reshape(g.shape[0] // (2 * tok), 2, tok, g.shape[1]) for g in grad_pieces]
    starts = starts // (2 * tok)
    lead_other = lax.ppermute(lead_all, "core", swap)
    trail_other = lax.ppermute(trail_all, "core", swap)
    part_mine = block_products(
        lead_all, trail_all, grad_pieces, starts, place, in_half, local_cols, use_mine, ny
    )
    part_other = block_products(
        lead_other, trail_other, grad_pieces, starts, place, in_half, local_cols, use_other, ny
    )
    totals = part_mine + part_other
    return totals.reshape(1, 1, MAXB, BLK, BLK)


def solution(mesh):
    n_in, n_out = mesh.devices.shape
    row = mesh.devices[0]
    ny = len({d.coords[1] for d in row})
    ncore = n_out // len({tuple(d.coords) for d in row})
    nz = n_out // (ny * ncore)
    split = jax.sharding.Mesh(
        mesh.devices.reshape(n_in, nz, ny, ncore), ("in", "z", "y", "core")
    )
    out = ("z", "y", "core")
    return jax.shard_map(
        on_device,
        mesh=split,
        in_specs=(
            P(out, "in"),
            P("in", out),
            P("in", out, None),
            P("in", out, None),
            P("in", out),
        ),
        out_specs=P("in", out, None, None, None),
        check_vma=False,
    )
```

```python
import functools

import jax
import jax.numpy as jnp
from jax import lax
from jax.experimental import pallas as pl
from jax.experimental.pallas import tpu as pltpu
from jax.sharding import PartitionSpec as P

BLK = 128
MAXB = 4


def block_kernel(n_grad, ny, rows_ref, cols_ref, use_ref, starts_ref, place_ref, *rest):
    act_hbm = rest[0]
    grad_hbm = rest[1:1 + n_grad]
    out_ref, a_v, g_v, sems = rest[1 + n_grad:]
    chunks, _, tok, _ = a_v.shape[1:]

    copies = []
    for s in range(MAXB):
        r = pl.multiple_of(rows_ref[s] * BLK, BLK)
        c = pl.multiple_of(cols_ref[s] * BLK, BLK)
        slot = [
            pltpu.make_async_copy(act_hbm.at[0, :, :, pl.ds(r, BLK)], a_v.at[s, :, 0], sems.at[s, 0]),
            pltpu.make_async_copy(act_hbm.at[1, :, :, pl.ds(r, BLK)], a_v.at[s, :, 1], sems.at[s, 1]),
        ]
        for p, piece in enumerate(grad_hbm):
            slot.append(
                pltpu.make_async_copy(
                    piece.at[:, :, :, pl.ds(c, BLK)],
                    g_v.at[s, pl.ds(starts_ref[p], piece.shape[0])],
                    sems.at[s, p + 2],
                )
            )

        @pl.when(use_ref[s] == 1)
        def _(slot=slot):
            for cp in slot:
                cp.start()

        copies.append(slot)

    z_me, y_me = place_ref[0], place_ref[1]
    nz = chunks // ny
    for s in range(MAXB):

        @pl.when(use_ref[s] == 0)
        def _(s=s):
            out_ref[s] = jnp.zeros((BLK, BLK), jnp.float32)

        @pl.when(use_ref[s] == 1)
        def _(s=s):
            for cp in copies[s]:
                cp.wait()

            def body(k, acc):
                pair = ((z_me + k // ny) % nz) * ny + (y_me + k % ny) % ny
                a = a_v[s, k].reshape(2 * tok, BLK)
                g = g_v[s, pair].reshape(2 * tok, BLK)
                return acc + lax.dot_general(
                    a, g, (((0,), (0,)), ((), ())), preferred_element_type=jnp.float32
                )

            out_ref[s] = lax.fori_loop(
                0, chunks, body, jnp.zeros((BLK, BLK), jnp.float32), unroll=8
            )


def block_products(both, grad_pieces, starts, place, local_rows, local_cols, use, ny):
    _, chunks, tok, width = both.shape
    n_grad = len(grad_pieces)
    smem = pl.BlockSpec(memory_space=pltpu.SMEM)
    hbm = pl.BlockSpec(memory_space=pl.ANY)
    tokens = 2 * chunks * tok
    flops = 2 * MAXB * tokens * BLK * BLK
    moved = 2 * MAXB * tokens * BLK * 2 + MAXB * BLK * BLK * 4
    return pl.pallas_call(
        functools.partial(block_kernel, n_grad, ny),
        out_shape=jax.ShapeDtypeStruct((MAXB, BLK, BLK), jnp.float32),
        in_specs=[smem] * 5 + [hbm] * (1 + n_grad),
        out_specs=pl.BlockSpec(memory_space=pltpu.VMEM),
        scratch_shapes=[
            pltpu.VMEM((MAXB, chunks, 2, tok, BLK), jnp.bfloat16),
            pltpu.VMEM((MAXB, chunks, 2, tok, BLK), jnp.bfloat16),
            pltpu.SemaphoreType.DMA((MAXB, 2 + n_grad)),
        ],
        compiler_params=pltpu.CompilerParams(vmem_limit_bytes=48 * 1024 * 1024),
        cost_estimate=pl.CostEstimate(flops=flops, bytes_accessed=moved, transcendentals=0),
    )(local_rows, local_cols, use, starts, place, both, *grad_pieces)


def relative_gather(x, axis, n, split=True):
    right = [(k, (k + 1) % n) for k in range(n)]
    left = [(k, (k - 1) % n) for k in range(n)]
    rel = [x] + [None] * (n - 1)
    from_left, from_right = x, x
    for t in range(1, (n + 1) // 2):
        from_left = lax.ppermute(from_left, axis, right)
        from_right = lax.ppermute(from_right, axis, left)
        rel[n - t] = from_left
        rel[t] = from_right
    if n % 2 == 0 and n > 1 and not split:
        rel[n // 2] = lax.ppermute(from_left, axis, right)
    elif n % 2 == 0 and n > 1:
        t = n // 2
        half = x.shape[0] // 2
        near_a = lax.ppermute(from_left[:half], axis, right)
        near_b = lax.ppermute(from_right[half:], axis, left)
        rel[t] = jnp.concatenate([near_a, near_b], 0)
    return rel


def ring_gather(own, axis, place):
    n = lax.axis_size(axis)
    length = own.shape[0]
    right = [(k, (k + 1) % n) for k in range(n)]
    left = [(k, (k - 1) % n) for k in range(n)]
    pieces, starts = [own], [place * length]
    from_left, from_right = own, own
    for d in range(1, (n + 1) // 2):
        from_left = lax.ppermute(from_left, axis, right)
        from_right = lax.ppermute(from_right, axis, left)
        pieces += [from_left, from_right]
        starts += [((place - d) % n) * length, ((place + d) % n) * length]
    if n % 2 == 0 and n > 1:
        half = length // 2
        d = n // 2
        if d == 1:
            near_a, near_b = lax.ppermute(own[:half], axis, right), lax.ppermute(own[half:], axis, left)
        else:
            near_a = lax.ppermute(from_left[:half], axis, right)
            near_b = lax.ppermute(from_right[half:], axis, left)
        far = ((place + d) % n) * length
        pieces += [near_a, near_b]
        starts += [far, far + half]
    return pieces, jnp.stack(starts).astype(jnp.int32)


def on_device(activations, out_grad, block_rows, block_cols, counts):
    in_place = lax.axis_index("in")
    core = lax.axis_index("core")
    nz, ny, ncore = lax.axis_size("z"), lax.axis_size("y"), lax.axis_size("core")
    z_me, y_me = lax.axis_index("z"), lax.axis_index("y")
    out_place = (z_me * ny + y_me) * ncore + core
    tok = activations.shape[0]
    tile_rows = activations.shape[1] // BLK
    tile_cols = out_grad.shape[1] // BLK
    half_rows = tile_rows // 2
    local_rows = jnp.clip(block_rows[0, 0] - in_place * tile_rows, 0, tile_rows - 1)
    local_cols = jnp.clip(block_cols[0, 0] - out_place * tile_cols, 0, tile_cols - 1)
    live = jnp.arange(MAXB, dtype=jnp.int32) < counts[0, 0]
    mine_half = (local_rows // half_rows) == core
    use_mine = (live & mine_half).astype(jnp.int32)
    use_other = (live & ~mine_half).astype(jnp.int32)
    in_half = (local_rows % half_rows).astype(jnp.int32)
    place = jnp.stack([z_me, y_me]).astype(jnp.int32)

    width = half_rows * BLK
    first, second = activations[:, :width], activations[:, width:]
    on_first = core == 0
    keep = jnp.where(on_first, first, second)
    send = jnp.where(on_first, second, first)
    swap = [(0, 1), (1, 0)]
    recv = lax.ppermute(send, "core", swap)
    lead = jnp.where(on_first, keep, recv)
    trail = jnp.where(on_first, recv, keep)

    lead_z = jnp.stack(relative_gather(lead, "z", nz, split=False), 0)
    lead_all = jnp.stack(relative_gather(lead_z, "y", ny), 1)
    trail_y = jnp.stack(relative_gather(trail, "y", ny, split=False), 0)
    trail_all = jnp.stack(relative_gather(trail_y, "z", nz), 0)
    lead_all = lead_all.reshape(nz * ny, tok, width)
    trail_all = trail_all.reshape(nz * ny, tok, width)

    grad_pieces, starts = ring_gather(out_grad, "in", in_place)
    both = jnp.stack([lead_all, trail_all], 0)
    both, grad_pieces = lax.optimization_barrier((both, grad_pieces))
    grad_pieces = [g.reshape(g.shape[0] // (2 * tok), 2, tok, g.shape[1]) for g in grad_pieces]
    starts = starts // (2 * tok)
    other = lax.ppermute(both, "core", swap)
    part_mine = block_products(both, grad_pieces, starts, place, in_half, local_cols, use_mine, ny)
    part_other = block_products(other, grad_pieces, starts, place, in_half, local_cols, use_other, ny)
    totals = part_mine + part_other
    return totals.reshape(1, 1, MAXB, BLK, BLK)


def solution(mesh):
    n_in, n_out = mesh.devices.shape
    row = mesh.devices[0]
    ny = len({d.coords[1] for d in row})
    ncore = n_out // len({tuple(d.coords) for d in row})
    nz = n_out // (ny * ncore)
    split = jax.sharding.Mesh(
        mesh.devices.reshape(n_in, nz, ny, ncore), ("in", "z", "y", "core")
    )
    out = ("z", "y", "core")
    return jax.shard_map(
        on_device,
        mesh=split,
        in_specs=(
            P(out, "in"),
            P("in", out),
            P("in", out, None),
            P("in", out, None),
            P("in", out),
        ),
        out_specs=P("in", out, None, None, None),
        check_vma=False,
    )
```

```python
import functools

import jax
import jax.numpy as jnp
from jax import lax
from jax.experimental import pallas as pl
from jax.experimental.pallas import tpu as pltpu
from jax.sharding import PartitionSpec as P

BLK = 128
MAXB = 4


def block_kernel(n_grad, ny, rows_ref, cols_ref, use_ref, starts_ref, place_ref, *rest):
    first_hbm, second_hbm = rest[0], rest[1]
    grad_hbm = rest[2:2 + n_grad]
    out_ref, a_v, g_v, sems = rest[2 + n_grad:]
    chunks, _, tok, _ = a_v.shape[1:]

    copies = []
    for s in range(MAXB):
        r = pl.multiple_of(rows_ref[s] * BLK, BLK)
        c = pl.multiple_of(cols_ref[s] * BLK, BLK)
        slot = [
            pltpu.make_async_copy(first_hbm.at[:, :, pl.ds(r, BLK)], a_v.at[s, :, 0], sems.at[s, 0]),
            pltpu.make_async_copy(second_hbm.at[:, :, pl.ds(r, BLK)], a_v.at[s, :, 1], sems.at[s, 1]),
        ]
        for p, piece in enumerate(grad_hbm):
            slot.append(
                pltpu.make_async_copy(
                    piece.at[:, :, :, pl.ds(c, BLK)],
                    g_v.at[s, pl.ds(starts_ref[p], piece.shape[0])],
                    sems.at[s, p + 2],
                )
            )

        @pl.when(use_ref[s] == 1)
        def _(slot=slot):
            for cp in slot:
                cp.start()

        copies.append(slot)

    z_me, y_me = place_ref[0], place_ref[1]
    nz = chunks // ny
    for s in range(MAXB):

        @pl.when(use_ref[s] == 0)
        def _(s=s):
            out_ref[s] = jnp.zeros((BLK, BLK), jnp.float32)

        @pl.when(use_ref[s] == 1)
        def _(s=s):
            for cp in copies[s]:
                cp.wait()

            def body(k, acc):
                pair = ((z_me + k // ny) % nz) * ny + (y_me + k % ny) % ny
                a = a_v[s, k].reshape(2 * tok, BLK)
                g = g_v[s, pair].reshape(2 * tok, BLK)
                return acc + lax.dot_general(
                    a, g, (((0,), (0,)), ((), ())), preferred_element_type=jnp.float32
                )

            out_ref[s] = lax.fori_loop(
                0, chunks, body, jnp.zeros((BLK, BLK), jnp.float32), unroll=8
            )


def block_products(first, second, grad_pieces, starts, place, local_rows, local_cols, use, ny):
    chunks, tok, width = first.shape
    n_grad = len(grad_pieces)
    smem = pl.BlockSpec(memory_space=pltpu.SMEM)
    hbm = pl.BlockSpec(memory_space=pl.ANY)
    tokens = 2 * chunks * tok
    flops = 2 * MAXB * tokens * BLK * BLK
    moved = 2 * MAXB * tokens * BLK * 2 + MAXB * BLK * BLK * 4
    return pl.pallas_call(
        functools.partial(block_kernel, n_grad, ny),
        out_shape=jax.ShapeDtypeStruct((MAXB, BLK, BLK), jnp.float32),
        in_specs=[smem] * 5 + [hbm] * (2 + n_grad),
        out_specs=pl.BlockSpec(memory_space=pltpu.VMEM),
        scratch_shapes=[
            pltpu.VMEM((MAXB, chunks, 2, tok, BLK), jnp.bfloat16),
            pltpu.VMEM((MAXB, chunks, 2, tok, BLK), jnp.bfloat16),
            pltpu.SemaphoreType.DMA((MAXB, 2 + n_grad)),
        ],
        compiler_params=pltpu.CompilerParams(vmem_limit_bytes=48 * 1024 * 1024),
        cost_estimate=pl.CostEstimate(flops=flops, bytes_accessed=moved, transcendentals=0),
    )(local_rows, local_cols, use, starts, place, first, second, *grad_pieces)


def relative_gather(x, axis, n, split=True):
    right = [(k, (k + 1) % n) for k in range(n)]
    left = [(k, (k - 1) % n) for k in range(n)]
    rel = [x] + [None] * (n - 1)
    from_left, from_right = x, x
    for t in range(1, (n + 1) // 2):
        from_left = lax.ppermute(from_left, axis, right)
        from_right = lax.ppermute(from_right, axis, left)
        rel[n - t] = from_left
        rel[t] = from_right
    if n % 2 == 0 and n > 1 and not split:
        rel[n // 2] = lax.ppermute(from_left, axis, right)
    elif n % 2 == 0 and n > 1:
        t = n // 2
        half = x.shape[0] // 2
        near_a = lax.ppermute(from_left[:half], axis, right)
        near_b = lax.ppermute(from_right[half:], axis, left)
        rel[t] = jnp.concatenate([near_a, near_b], 0)
    return rel


def ring_gather(own, axis, place):
    n = lax.axis_size(axis)
    length = own.shape[0]
    right = [(k, (k + 1) % n) for k in range(n)]
    left = [(k, (k - 1) % n) for k in range(n)]
    pieces, starts = [own], [place * length]
    from_left, from_right = own, own
    for d in range(1, (n + 1) // 2):
        from_left = lax.ppermute(from_left, axis, right)
        from_right = lax.ppermute(from_right, axis, left)
        pieces += [from_left, from_right]
        starts += [((place - d) % n) * length, ((place + d) % n) * length]
    if n % 2 == 0 and n > 1:
        half = length // 2
        d = n // 2
        if d == 1:
            near_a, near_b = lax.ppermute(own[:half], axis, right), lax.ppermute(own[half:], axis, left)
        else:
            near_a = lax.ppermute(from_left[:half], axis, right)
            near_b = lax.ppermute(from_right[half:], axis, left)
        far = ((place + d) % n) * length
        pieces += [near_a, near_b]
        starts += [far, far + half]
    return pieces, jnp.stack(starts).astype(jnp.int32)


def on_device(activations, out_grad, block_rows, block_cols, counts):
    in_place = lax.axis_index("in")
    core = lax.axis_index("core")
    nz, ny, ncore = lax.axis_size("z"), lax.axis_size("y"), lax.axis_size("core")
    z_me, y_me = lax.axis_index("z"), lax.axis_index("y")
    out_place = (z_me * ny + y_me) * ncore + core
    tok = activations.shape[0]
    tile_rows = activations.shape[1] // BLK
    tile_cols = out_grad.shape[1] // BLK
    half_rows = tile_rows // 2
    local_rows = jnp.clip(block_rows[0, 0] - in_place * tile_rows, 0, tile_rows - 1)
    local_cols = jnp.clip(block_cols[0, 0] - out_place * tile_cols, 0, tile_cols - 1)
    live = jnp.arange(MAXB, dtype=jnp.int32) < counts[0, 0]
    mine_half = (local_rows // half_rows) == core
    use_mine = (live & mine_half).astype(jnp.int32)
    use_other = (live & ~mine_half).astype(jnp.int32)
    in_half = (local_rows % half_rows).astype(jnp.int32)
    place = jnp.stack([z_me, y_me]).astype(jnp.int32)

    width = half_rows * BLK
    first, second = activations[:, :width], activations[:, width:]
    on_first = core == 0
    keep = jnp.where(on_first, first, second)
    send = jnp.where(on_first, second, first)
    swap = [(0, 1), (1, 0)]
    recv = lax.ppermute(send, "core", swap)
    lead = jnp.where(on_first, keep, recv)
    trail = jnp.where(on_first, recv, keep)

    lead_z = jnp.stack(relative_gather(lead, "z", nz, split=False), 0)
    lead_all = jnp.stack(relative_gather(lead_z, "y", ny), 1)
    trail_y = jnp.stack(relative_gather(trail, "y", ny, split=False), 0)
    trail_all = jnp.stack(relative_gather(trail_y, "z", nz), 0)
    lead_all = lead_all.reshape(nz * ny, tok, width)
    trail_all = trail_all.reshape(nz * ny, tok, width)

    grad_pieces, starts = ring_gather(out_grad, "in", in_place)
    lead_all, trail_all, grad_pieces = lax.optimization_barrier((lead_all, trail_all, grad_pieces))
    grad_pieces = [g.reshape(g.shape[0] // (2 * tok), 2, tok, g.shape[1]) for g in grad_pieces]
    starts = starts // (2 * tok)
    lead_other = lax.ppermute(lead_all, "core", swap)
    trail_other = lax.ppermute(trail_all, "core", swap)
    part_mine = block_products(
        lead_all, trail_all, grad_pieces, starts, place, in_half, local_cols, use_mine, ny
    )
    part_other = block_products(
        lead_other, trail_other, grad_pieces, starts, place, in_half, local_cols, use_other, ny
    )
    totals = part_mine + part_other
    return totals.reshape(1, 1, MAXB, BLK, BLK)


def solution(mesh):
    n_in, n_out = mesh.devices.shape
    row = mesh.devices[0]
    ny = len({d.coords[1] for d in row})
    ncore = n_out // len({tuple(d.coords) for d in row})
    nz = n_out // (ny * ncore)
    split = jax.sharding.Mesh(
        mesh.devices.reshape(n_in, nz, ny, ncore), ("in", "z", "y", "core")
    )
    out = ("z", "y", "core")
    return jax.shard_map(
        on_device,
        mesh=split,
        in_specs=(
            P(out, "in"),
            P("in", out),
            P("in", out, None),
            P("in", out, None),
            P("in", out),
        ),
        out_specs=P("in", out, None, None, None),
        check_vma=False,
    )
```

```python
import functools

import jax
import jax.numpy as jnp
from jax import lax
from jax.experimental import pallas as pl
from jax.experimental.pallas import tpu as pltpu
from jax.sharding import PartitionSpec as P

BLK = 128
MAXB = 4


def block_kernel(n_grad, ny, rows_ref, cols_ref, use_ref, starts_ref, place_ref, *rest):
    first_hbm, second_hbm = rest[0], rest[1]
    grad_hbm = rest[2:2 + n_grad]
    out_ref, a_v, g_v, sems = rest[2 + n_grad:]
    chunks, _, tok, _ = a_v.shape[1:]

    copies = []
    for s in range(MAXB):
        r = pl.multiple_of(rows_ref[s] * BLK, BLK)
        c = pl.multiple_of(cols_ref[s] * BLK, BLK)
        slot = [
            pltpu.make_async_copy(first_hbm.at[:, :, pl.ds(r, BLK)], a_v.at[s, :, 0], sems.at[s, 0]),
            pltpu.make_async_copy(second_hbm.at[:, :, pl.ds(r, BLK)], a_v.at[s, :, 1], sems.at[s, 1]),
        ]
        for p, piece in enumerate(grad_hbm):
            slot.append(
                pltpu.make_async_copy(
                    piece.at[:, :, :, pl.ds(c, BLK)],
                    g_v.at[s, pl.ds(starts_ref[p], piece.shape[0])],
                    sems.at[s, p + 2],
                )
            )

        @pl.when(use_ref[s] == 1)
        def _(slot=slot):
            for cp in slot:
                cp.start()

        copies.append(slot)

    z_me, y_me = place_ref[0], place_ref[1]
    nz = chunks // ny
    for s in range(MAXB):

        @pl.when(use_ref[s] == 0)
        def _(s=s):
            out_ref[s] = jnp.zeros((BLK, BLK), jnp.float32)

        @pl.when(use_ref[s] == 1)
        def _(s=s):
            for cp in copies[s]:
                cp.wait()

            def body(k, acc):
                pair = ((z_me + k // ny) % nz) * ny + (y_me + k % ny) % ny
                a = a_v[s, k].reshape(2 * tok, BLK)
                g = g_v[s, pair].reshape(2 * tok, BLK)
                return acc + lax.dot_general(
                    a, g, (((0,), (0,)), ((), ())), preferred_element_type=jnp.float32
                )

            out_ref[s] = lax.fori_loop(
                0, chunks, body, jnp.zeros((BLK, BLK), jnp.float32), unroll=8
            )


def block_products(first, second, grad_pieces, starts, place, local_rows, local_cols, use, ny):
    chunks, tok, width = first.shape
    n_grad = len(grad_pieces)
    smem = pl.BlockSpec(memory_space=pltpu.SMEM)
    hbm = pl.BlockSpec(memory_space=pl.ANY)
    tokens = 2 * chunks * tok
    flops = 2 * MAXB * tokens * BLK * BLK
    moved = 2 * MAXB * tokens * BLK * 2 + MAXB * BLK * BLK * 4
    return pl.pallas_call(
        functools.partial(block_kernel, n_grad, ny),
        out_shape=jax.ShapeDtypeStruct((MAXB, BLK, BLK), jnp.float32),
        in_specs=[smem] * 5 + [hbm] * (2 + n_grad),
        out_specs=pl.BlockSpec(memory_space=pltpu.VMEM),
        scratch_shapes=[
            pltpu.VMEM((MAXB, chunks, 2, tok, BLK), jnp.bfloat16),
            pltpu.VMEM((MAXB, chunks, 2, tok, BLK), jnp.bfloat16),
            pltpu.SemaphoreType.DMA((MAXB, 2 + n_grad)),
        ],
        compiler_params=pltpu.CompilerParams(vmem_limit_bytes=48 * 1024 * 1024),
        cost_estimate=pl.CostEstimate(flops=flops, bytes_accessed=moved, transcendentals=0),
    )(local_rows, local_cols, use, starts, place, first, second, *grad_pieces)


def relative_gather(x, axis, n, split=True):
    right = [(k, (k + 1) % n) for k in range(n)]
    left = [(k, (k - 1) % n) for k in range(n)]
    rel = [x] + [None] * (n - 1)
    from_left, from_right = x, x
    for t in range(1, (n + 1) // 2):
        from_left = lax.ppermute(from_left, axis, right)
        from_right = lax.ppermute(from_right, axis, left)
        rel[n - t] = from_left
        rel[t] = from_right
    if n % 2 == 0 and n > 1 and not split:
        rel[n // 2] = lax.ppermute(from_left, axis, right)
    elif n % 2 == 0 and n > 1:
        t = n // 2
        half = x.shape[0] // 2
        near_a = lax.ppermute(from_left[:half], axis, right)
        near_b = lax.ppermute(from_right[half:], axis, left)
        rel[t] = jnp.concatenate([near_a, near_b], 0)
    return rel


def ring_gather(own, axis, place):
    n = lax.axis_size(axis)
    length = own.shape[0]
    right = [(k, (k + 1) % n) for k in range(n)]
    left = [(k, (k - 1) % n) for k in range(n)]
    pieces, starts = [own], [place * length]
    from_left, from_right = own, own
    for d in range(1, (n + 1) // 2):
        from_left = lax.ppermute(from_left, axis, right)
        from_right = lax.ppermute(from_right, axis, left)
        pieces += [from_left, from_right]
        starts += [((place - d) % n) * length, ((place + d) % n) * length]
    if n % 2 == 0 and n > 1:
        half = length // 2
        d = n // 2
        if d == 1:
            near_a, near_b = lax.ppermute(own[:half], axis, right), lax.ppermute(own[half:], axis, left)
        else:
            near_a = lax.ppermute(from_left[:half], axis, right)
            near_b = lax.ppermute(from_right[half:], axis, left)
        far = ((place + d) % n) * length
        pieces += [near_a, near_b]
        starts += [far, far + half]
    return pieces, jnp.stack(starts).astype(jnp.int32)


def on_device(activations, out_grad, block_rows, block_cols, counts):
    in_place = lax.axis_index("in")
    core = lax.axis_index("core")
    nz, ny, ncore = lax.axis_size("z"), lax.axis_size("y"), lax.axis_size("core")
    z_me, y_me = lax.axis_index("z"), lax.axis_index("y")
    out_place = (z_me * ny + y_me) * ncore + core
    tok = activations.shape[0]
    tile_rows = activations.shape[1] // BLK
    tile_cols = out_grad.shape[1] // BLK
    half_rows = tile_rows // 2
    local_rows = jnp.clip(block_rows[0, 0] - in_place * tile_rows, 0, tile_rows - 1)
    local_cols = jnp.clip(block_cols[0, 0] - out_place * tile_cols, 0, tile_cols - 1)
    live = jnp.arange(MAXB, dtype=jnp.int32) < counts[0, 0]
    mine_half = (local_rows // half_rows) == core
    use_mine = (live & mine_half).astype(jnp.int32)
    use_other = (live & ~mine_half).astype(jnp.int32)
    in_half = (local_rows % half_rows).astype(jnp.int32)
    place = jnp.stack([z_me, y_me]).astype(jnp.int32)

    width = half_rows * BLK
    first, second = activations[:, :width], activations[:, width:]
    on_first = core == 0
    keep = jnp.where(on_first, first, second)
    send = jnp.where(on_first, second, first)
    swap = [(0, 1), (1, 0)]
    recv = lax.ppermute(send, "core", swap)
    lead = jnp.where(on_first, keep, recv)
    trail = jnp.where(on_first, recv, keep)

    lead_z = jnp.stack(relative_gather(lead, "z", nz, split=False), 0)
    trail_y = jnp.stack(relative_gather(trail, "y", ny, split=False), 0)
    grad_pieces, starts = ring_gather(out_grad, "in", in_place)
    lead_z, trail_y, grad_pieces = lax.optimization_barrier((lead_z, trail_y, grad_pieces))
    lead_all = jnp.stack(relative_gather(lead_z, "y", ny), 1)
    trail_all = jnp.stack(relative_gather(trail_y, "z", nz), 0)
    lead_all = lead_all.reshape(nz * ny, tok, width)
    trail_all = trail_all.reshape(nz * ny, tok, width)

    lead_all, trail_all, grad_pieces = lax.optimization_barrier((lead_all, trail_all, grad_pieces))
    grad_pieces = [g.reshape(g.shape[0] // (2 * tok), 2, tok, g.shape[1]) for g in grad_pieces]
    starts = starts // (2 * tok)
    lead_other = lax.ppermute(lead_all, "core", swap)
    trail_other = lax.ppermute(trail_all, "core", swap)
    part_mine = block_products(
        lead_all, trail_all, grad_pieces, starts, place, in_half, local_cols, use_mine, ny
    )
    part_other = block_products(
        lead_other, trail_other, grad_pieces, starts, place, in_half, local_cols, use_other, ny
    )
    totals = part_mine + part_other
    return totals.reshape(1, 1, MAXB, BLK, BLK)


def solution(mesh):
    n_in, n_out = mesh.devices.shape
    row = mesh.devices[0]
    ny = len({d.coords[1] for d in row})
    ncore = n_out // len({tuple(d.coords) for d in row})
    nz = n_out // (ny * ncore)
    split = jax.sharding.Mesh(
        mesh.devices.reshape(n_in, nz, ny, ncore), ("in", "z", "y", "core")
    )
    out = ("z", "y", "core")
    return jax.shard_map(
        on_device,
        mesh=split,
        in_specs=(
            P(out, "in"),
            P("in", out),
            P("in", out, None),
            P("in", out, None),
            P("in", out),
        ),
        out_specs=P("in", out, None, None, None),
        check_vma=False,
    )
```

```python
import functools

import jax
import jax.numpy as jnp
from jax import lax
from jax.experimental import pallas as pl
from jax.experimental.pallas import tpu as pltpu
from jax.sharding import PartitionSpec as P

BLK = 128
MAXB = 4


def block_kernel(n_grad, ny, rows_ref, cols_ref, use_ref, starts_ref, place_ref, *rest):
    first_hbm, second_hbm = rest[0], rest[1]
    grad_hbm = rest[2:2 + n_grad]
    out_ref, a_v, g_v, sems = rest[2 + n_grad:]
    chunks, _, tok, _ = a_v.shape[1:]

    copies = []
    for s in range(MAXB):
        r = pl.multiple_of(rows_ref[s] * BLK, BLK)
        c = pl.multiple_of(cols_ref[s] * BLK, BLK)
        slot = [
            pltpu.make_async_copy(first_hbm.at[:, :, pl.ds(r, BLK)], a_v.at[s, :, 0], sems.at[s, 0]),
            pltpu.make_async_copy(second_hbm.at[:, :, pl.ds(r, BLK)], a_v.at[s, :, 1], sems.at[s, 1]),
        ]
        for p, piece in enumerate(grad_hbm):
            slot.append(
                pltpu.make_async_copy(
                    piece.at[:, :, :, pl.ds(c, BLK)],
                    g_v.at[s, pl.ds(starts_ref[p], piece.shape[0])],
                    sems.at[s, p + 2],
                )
            )

        @pl.when(use_ref[s] == 1)
        def _(slot=slot):
            for cp in slot:
                cp.start()

        copies.append(slot)

    z_me, y_me = place_ref[0], place_ref[1]
    nz = chunks // ny
    for s in range(MAXB):

        @pl.when(use_ref[s] == 0)
        def _(s=s):
            out_ref[s] = jnp.zeros((BLK, BLK), jnp.float32)

        @pl.when(use_ref[s] == 1)
        def _(s=s):
            for cp in copies[s]:
                cp.wait()

            def body(k, acc):
                pair = ((z_me + k // ny) % nz) * ny + (y_me + k % ny) % ny
                a = a_v[s, k].reshape(2 * tok, BLK)
                g = g_v[s, pair].reshape(2 * tok, BLK)
                return acc + lax.dot_general(
                    a, g, (((0,), (0,)), ((), ())), preferred_element_type=jnp.float32
                )

            out_ref[s] = lax.fori_loop(
                0, chunks, body, jnp.zeros((BLK, BLK), jnp.float32), unroll=True
            )


def block_products(first, second, grad_pieces, starts, place, local_rows, local_cols, use, ny):
    chunks, tok, width = first.shape
    n_grad = len(grad_pieces)
    smem = pl.BlockSpec(memory_space=pltpu.SMEM)
    hbm = pl.BlockSpec(memory_space=pl.ANY)
    tokens = 2 * chunks * tok
    flops = 2 * MAXB * tokens * BLK * BLK
    moved = 2 * MAXB * tokens * BLK * 2 + MAXB * BLK * BLK * 4
    return pl.pallas_call(
        functools.partial(block_kernel, n_grad, ny),
        out_shape=jax.ShapeDtypeStruct((MAXB, BLK, BLK), jnp.float32),
        in_specs=[smem] * 5 + [hbm] * (2 + n_grad),
        out_specs=pl.BlockSpec(memory_space=pltpu.VMEM),
        scratch_shapes=[
            pltpu.VMEM((MAXB, chunks, 2, tok, BLK), jnp.bfloat16),
            pltpu.VMEM((MAXB, chunks, 2, tok, BLK), jnp.bfloat16),
            pltpu.SemaphoreType.DMA((MAXB, 2 + n_grad)),
        ],
        compiler_params=pltpu.CompilerParams(vmem_limit_bytes=48 * 1024 * 1024),
        cost_estimate=pl.CostEstimate(flops=flops, bytes_accessed=moved, transcendentals=0),
    )(local_rows, local_cols, use, starts, place, first, second, *grad_pieces)


def relative_gather(x, axis, n, split=True):
    right = [(k, (k + 1) % n) for k in range(n)]
    left = [(k, (k - 1) % n) for k in range(n)]
    rel = [x] + [None] * (n - 1)
    from_left, from_right = x, x
    for t in range(1, (n + 1) // 2):
        from_left = lax.ppermute(from_left, axis, right)
        from_right = lax.ppermute(from_right, axis, left)
        rel[n - t] = from_left
        rel[t] = from_right
    if n % 2 == 0 and n > 1 and not split:
        rel[n // 2] = lax.ppermute(from_left, axis, right)
    elif n % 2 == 0 and n > 1:
        t = n // 2
        half = x.shape[0] // 2
        near_a = lax.ppermute(from_left[:half], axis, right)
        near_b = lax.ppermute(from_right[half:], axis, left)
        rel[t] = jnp.concatenate([near_a, near_b], 0)
    return rel


def ring_gather(own, axis, place):
    n = lax.axis_size(axis)
    length = own.shape[0]
    right = [(k, (k + 1) % n) for k in range(n)]
    left = [(k, (k - 1) % n) for k in range(n)]
    pieces, starts = [own], [place * length]
    from_left, from_right = own, own
    for d in range(1, (n + 1) // 2):
        from_left = lax.ppermute(from_left, axis, right)
        from_right = lax.ppermute(from_right, axis, left)
        pieces += [from_left, from_right]
        starts += [((place - d) % n) * length, ((place + d) % n) * length]
    if n % 2 == 0 and n > 1:
        half = length // 2
        d = n // 2
        if d == 1:
            near_a, near_b = lax.ppermute(own[:half], axis, right), lax.ppermute(own[half:], axis, left)
        else:
            near_a = lax.ppermute(from_left[:half], axis, right)
            near_b = lax.ppermute(from_right[half:], axis, left)
        far = ((place + d) % n) * length
        pieces += [near_a, near_b]
        starts += [far, far + half]
    return pieces, jnp.stack(starts).astype(jnp.int32)


def on_device(activations, out_grad, block_rows, block_cols, counts):
    in_place = lax.axis_index("in")
    core = lax.axis_index("core")
    nz, ny, ncore = lax.axis_size("z"), lax.axis_size("y"), lax.axis_size("core")
    z_me, y_me = lax.axis_index("z"), lax.axis_index("y")
    out_place = (z_me * ny + y_me) * ncore + core
    tok = activations.shape[0]
    tile_rows = activations.shape[1] // BLK
    tile_cols = out_grad.shape[1] // BLK
    half_rows = tile_rows // 2
    local_rows = jnp.clip(block_rows[0, 0] - in_place * tile_rows, 0, tile_rows - 1)
    local_cols = jnp.clip(block_cols[0, 0] - out_place * tile_cols, 0, tile_cols - 1)
    live = jnp.arange(MAXB, dtype=jnp.int32) < counts[0, 0]
    mine_half = (local_rows // half_rows) == core
    use_mine = (live & mine_half).astype(jnp.int32)
    use_other = (live & ~mine_half).astype(jnp.int32)
    in_half = (local_rows % half_rows).astype(jnp.int32)
    place = jnp.stack([z_me, y_me]).astype(jnp.int32)

    width = half_rows * BLK
    first, second = activations[:, :width], activations[:, width:]
    on_first = core == 0
    keep = jnp.where(on_first, first, second)
    send = jnp.where(on_first, second, first)
    swap = [(0, 1), (1, 0)]
    recv = lax.ppermute(send, "core", swap)
    lead = jnp.where(on_first, keep, recv)
    trail = jnp.where(on_first, recv, keep)

    lead_z = jnp.stack(relative_gather(lead, "z", nz, split=False), 0)
    lead_all = jnp.stack(relative_gather(lead_z, "y", ny), 1)
    trail_y = jnp.stack(relative_gather(trail, "y", ny, split=False), 0)
    trail_all = jnp.stack(relative_gather(trail_y, "z", nz), 0)
    lead_all = lead_all.reshape(nz * ny, tok, width)
    trail_all = trail_all.reshape(nz * ny, tok, width)

    grad_pieces, starts = ring_gather(out_grad, "in", in_place)
    lead_all, trail_all, grad_pieces = lax.optimization_barrier((lead_all, trail_all, grad_pieces))
    grad_pieces = [g.reshape(g.shape[0] // (2 * tok), 2, tok, g.shape[1]) for g in grad_pieces]
    starts = starts // (2 * tok)
    lead_other = lax.ppermute(lead_all, "core", swap)
    trail_other = lax.ppermute(trail_all, "core", swap)
    part_mine = block_products(
        lead_all, trail_all, grad_pieces, starts, place, in_half, local_cols, use_mine, ny
    )
    part_other = block_products(
        lead_other, trail_other, grad_pieces, starts, place, in_half, local_cols, use_other, ny
    )
    totals = part_mine + part_other
    return totals.reshape(1, 1, MAXB, BLK, BLK)


def solution(mesh):
    n_in, n_out = mesh.devices.shape
    row = mesh.devices[0]
    ny = len({d.coords[1] for d in row})
    ncore = n_out // len({tuple(d.coords) for d in row})
    nz = n_out // (ny * ncore)
    split = jax.sharding.Mesh(
        mesh.devices.reshape(n_in, nz, ny, ncore), ("in", "z", "y", "core")
    )
    out = ("z", "y", "core")
    return jax.shard_map(
        on_device,
        mesh=split,
        in_specs=(
            P(out, "in"),
            P("in", out),
            P("in", out, None),
            P("in", out, None),
            P("in", out),
        ),
        out_specs=P("in", out, None, None, None),
        check_vma=False,
    )
```

```python
import functools

import jax
import jax.numpy as jnp
from jax import lax
from jax.experimental import pallas as pl
from jax.experimental.pallas import tpu as pltpu
from jax.sharding import PartitionSpec as P

BLK = 128
MAXB = 4


def block_kernel(n_grad, ny, rows_ref, cols_ref, use_ref, starts_ref, place_ref, *rest):
    first_hbm, second_hbm = rest[0], rest[1]
    grad_hbm = rest[2:2 + n_grad]
    out_ref, a_v, g_v, sems = rest[2 + n_grad:]
    chunks, _, tok, _ = a_v.shape[1:]

    copies = []
    for s in range(MAXB):
        r = pl.multiple_of(rows_ref[s] * BLK, BLK)
        c = pl.multiple_of(cols_ref[s] * BLK, BLK)
        slot = [
            pltpu.make_async_copy(first_hbm.at[:, :, pl.ds(r, BLK)], a_v.at[s, :, 0], sems.at[s, 0]),
            pltpu.make_async_copy(second_hbm.at[:, :, pl.ds(r, BLK)], a_v.at[s, :, 1], sems.at[s, 1]),
        ]
        for p, piece in enumerate(grad_hbm):
            slot.append(
                pltpu.make_async_copy(
                    piece.at[:, :, :, pl.ds(c, BLK)],
                    g_v.at[s, pl.ds(starts_ref[p], piece.shape[0])],
                    sems.at[s, p + 2],
                )
            )

        @pl.when(use_ref[s] == 1)
        def _(slot=slot):
            for cp in slot:
                cp.start()

        copies.append(slot)

    z_me, y_me = place_ref[0], place_ref[1]
    nz = chunks // ny
    for s in range(MAXB):

        @pl.when(use_ref[s] == 0)
        def _(s=s):
            out_ref[s] = jnp.zeros((BLK, BLK), jnp.float32)

        @pl.when(use_ref[s] == 1)
        def _(s=s):
            for cp in copies[s]:
                cp.wait()

            def body(k, acc):
                pair = ((z_me + k // ny) % nz) * ny + (y_me + k % ny) % ny
                a = a_v[s, k].reshape(2 * tok, BLK)
                g = g_v[s, pair].reshape(2 * tok, BLK)
                return acc + lax.dot_general(
                    a, g, (((0,), (0,)), ((), ())), preferred_element_type=jnp.float32
                )

            out_ref[s] = lax.fori_loop(
                0, chunks, body, jnp.zeros((BLK, BLK), jnp.float32), unroll=8
            )


def block_products(first, second, grad_pieces, starts, place, local_rows, local_cols, use, ny):
    chunks, tok, width = first.shape
    n_grad = len(grad_pieces)
    smem = pl.BlockSpec(memory_space=pltpu.SMEM)
    hbm = pl.BlockSpec(memory_space=pl.ANY)
    tokens = 2 * chunks * tok
    flops = 2 * MAXB * tokens * BLK * BLK
    moved = 2 * MAXB * tokens * BLK * 2 + MAXB * BLK * BLK * 4
    return pl.pallas_call(
        functools.partial(block_kernel, n_grad, ny),
        out_shape=jax.ShapeDtypeStruct((MAXB, BLK, BLK), jnp.float32),
        in_specs=[smem] * 5 + [hbm] * (2 + n_grad),
        out_specs=pl.BlockSpec(memory_space=pltpu.VMEM),
        scratch_shapes=[
            pltpu.VMEM((MAXB, chunks, 2, tok, BLK), jnp.bfloat16),
            pltpu.VMEM((MAXB, chunks, 2, tok, BLK), jnp.bfloat16),
            pltpu.SemaphoreType.DMA((MAXB, 2 + n_grad)),
        ],
        compiler_params=pltpu.CompilerParams(vmem_limit_bytes=48 * 1024 * 1024),
        cost_estimate=pl.CostEstimate(flops=flops, bytes_accessed=moved, transcendentals=0),
    )(local_rows, local_cols, use, starts, place, first, second, *grad_pieces)


def relative_gather(x, axis, n, split=True):
    right = [(k, (k + 1) % n) for k in range(n)]
    left = [(k, (k - 1) % n) for k in range(n)]
    rel = [x] + [None] * (n - 1)
    from_left, from_right = x, x
    for t in range(1, (n + 1) // 2):
        from_left = lax.ppermute(from_left, axis, right)
        from_right = lax.ppermute(from_right, axis, left)
        rel[n - t] = from_left
        rel[t] = from_right
    if n % 2 == 0 and n > 1 and not split:
        rel[n // 2] = lax.ppermute(from_left, axis, right)
    elif n % 2 == 0 and n > 1:
        t = n // 2
        half = x.shape[0] // 2
        near_a = lax.ppermute(from_left[:half], axis, right)
        near_b = lax.ppermute(from_right[half:], axis, left)
        rel[t] = jnp.concatenate([near_a, near_b], 0)
    return rel


def ring_gather(own, axis, place):
    n = lax.axis_size(axis)
    length = own.shape[0]
    right = [(k, (k + 1) % n) for k in range(n)]
    left = [(k, (k - 1) % n) for k in range(n)]
    pieces, starts = [own], [place * length]
    from_left, from_right = own, own
    for d in range(1, (n + 1) // 2):
        from_left = lax.ppermute(from_left, axis, right)
        from_right = lax.ppermute(from_right, axis, left)
        pieces += [from_left, from_right]
        starts += [((place - d) % n) * length, ((place + d) % n) * length]
    if n % 2 == 0 and n > 1:
        half = length // 2
        d = n // 2
        if d == 1:
            near_a, near_b = lax.ppermute(own[:half], axis, right), lax.ppermute(own[half:], axis, left)
        else:
            near_a = lax.ppermute(from_left[:half], axis, right)
            near_b = lax.ppermute(from_right[half:], axis, left)
        far = ((place + d) % n) * length
        pieces += [near_a, near_b]
        starts += [far, far + half]
    return pieces, jnp.stack(starts).astype(jnp.int32)


def on_device(activations, out_grad, block_rows, block_cols, counts):
    in_place = lax.axis_index("in")
    core = lax.axis_index("core")
    nz, ny, ncore = lax.axis_size("z"), lax.axis_size("y"), lax.axis_size("core")
    z_me, y_me = lax.axis_index("z"), lax.axis_index("y")
    out_place = (z_me * ny + y_me) * ncore + core
    tok = activations.shape[0]
    tile_rows = activations.shape[1] // BLK
    tile_cols = out_grad.shape[1] // BLK
    half_rows = tile_rows // 2
    local_rows = jnp.clip(block_rows[0, 0] - in_place * tile_rows, 0, tile_rows - 1)
    local_cols = jnp.clip(block_cols[0, 0] - out_place * tile_cols, 0, tile_cols - 1)
    live = jnp.arange(MAXB, dtype=jnp.int32) < counts[0, 0]
    mine_half = (local_rows // half_rows) == core
    use_mine = (live & mine_half).astype(jnp.int32)
    use_other = (live & ~mine_half).astype(jnp.int32)
    in_half = (local_rows % half_rows).astype(jnp.int32)
    place = jnp.stack([z_me, y_me]).astype(jnp.int32)

    width = half_rows * BLK
    first, second = activations[:, :width], activations[:, width:]
    on_first = core == 0
    keep = jnp.where(on_first, first, second)
    send = jnp.where(on_first, second, first)
    swap = [(0, 1), (1, 0)]
    recv = lax.ppermute(send, "core", swap)
    lead = jnp.where(on_first, keep, recv)
    trail = jnp.where(on_first, recv, keep)

    lead_z = jnp.stack(relative_gather(lead, "z", nz, split=False), 0)
    trail_y = jnp.stack(relative_gather(trail, "y", ny, split=False), 0)
    n_in = lax.axis_size("in")
    length = out_grad.shape[0]
    right = [(k, (k + 1) % n_in) for k in range(n_in)]
    left = [(k, (k - 1) % n_in) for k in range(n_in)]
    from_left = lax.ppermute(out_grad, "in", right)
    from_right = lax.ppermute(out_grad, "in", left)
    lead_z, trail_y, from_left, from_right = lax.optimization_barrier(
        (lead_z, trail_y, from_left, from_right)
    )
    grad_pieces = [out_grad, from_left, from_right]
    offsets = [0, -1, 1]
    for d in range(2, n_in // 2 + 1):
        from_left = lax.ppermute(from_left, "in", right)
        grad_pieces.append(from_left)
        offsets.append(-d)
        if 2 * d < n_in:
            from_right = lax.ppermute(from_right, "in", left)
            grad_pieces.append(from_right)
            offsets.append(d)
    starts = jnp.stack([((in_place + o) % n_in) * length for o in offsets]).astype(jnp.int32)
    lead_all = jnp.stack(relative_gather(lead_z, "y", ny), 1)
    trail_all = jnp.stack(relative_gather(trail_y, "z", nz), 0)
    lead_all = lead_all.reshape(nz * ny, tok, width)
    trail_all = trail_all.reshape(nz * ny, tok, width)

    lead_all, trail_all, grad_pieces = lax.optimization_barrier((lead_all, trail_all, grad_pieces))
    grad_pieces = [g.reshape(g.shape[0] // (2 * tok), 2, tok, g.shape[1]) for g in grad_pieces]
    starts = starts // (2 * tok)
    lead_other = lax.ppermute(lead_all, "core", swap)
    trail_other = lax.ppermute(trail_all, "core", swap)
    part_mine = block_products(
        lead_all, trail_all, grad_pieces, starts, place, in_half, local_cols, use_mine, ny
    )
    part_other = block_products(
        lead_other, trail_other, grad_pieces, starts, place, in_half, local_cols, use_other, ny
    )
    totals = part_mine + part_other
    return totals.reshape(1, 1, MAXB, BLK, BLK)


def solution(mesh):
    n_in, n_out = mesh.devices.shape
    row = mesh.devices[0]
    ny = len({d.coords[1] for d in row})
    ncore = n_out // len({tuple(d.coords) for d in row})
    nz = n_out // (ny * ncore)
    split = jax.sharding.Mesh(
        mesh.devices.reshape(n_in, nz, ny, ncore), ("in", "z", "y", "core")
    )
    out = ("z", "y", "core")
    return jax.shard_map(
        on_device,
        mesh=split,
        in_specs=(
            P(out, "in"),
            P("in", out),
            P("in", out, None),
            P("in", out, None),
            P("in", out),
        ),
        out_specs=P("in", out, None, None, None),
        check_vma=False,
    )
```

```python
import functools

import jax
import jax.numpy as jnp
from jax import lax
from jax.experimental import pallas as pl
from jax.experimental.pallas import tpu as pltpu
from jax.sharding import PartitionSpec as P

BLK = 128
MAXB = 4


def block_kernel(n_grad, ny, rows_ref, cols_ref, use_ref, starts_ref, place_ref, *rest):
    first_hbm, second_hbm = rest[0], rest[1]
    grad_hbm = rest[2:2 + n_grad]
    out_ref, a_v, g_v, sems = rest[2 + n_grad:]
    chunks, _, tok, _ = a_v.shape[1:]

    copies = []
    for s in range(MAXB):
        r = pl.multiple_of(rows_ref[s] * BLK, BLK)
        c = pl.multiple_of(cols_ref[s] * BLK, BLK)
        slot = [
            pltpu.make_async_copy(first_hbm.at[:, :, pl.ds(r, BLK)], a_v.at[s, :, 0], sems.at[s, 0]),
            pltpu.make_async_copy(second_hbm.at[:, :, pl.ds(r, BLK)], a_v.at[s, :, 1], sems.at[s, 1]),
        ]
        for p, piece in enumerate(grad_hbm):
            slot.append(
                pltpu.make_async_copy(
                    piece.at[:, :, :, pl.ds(c, BLK)],
                    g_v.at[s, pl.ds(starts_ref[p], piece.shape[0])],
                    sems.at[s, p + 2],
                )
            )

        @pl.when(use_ref[s] == 1)
        def _(slot=slot):
            for cp in slot:
                cp.start()

        copies.append(slot)

    z_me, y_me = place_ref[0], place_ref[1]
    nz = chunks // ny
    for s in range(MAXB):

        @pl.when(use_ref[s] == 0)
        def _(s=s):
            out_ref[s] = jnp.zeros((BLK, BLK), jnp.float32)

        @pl.when(use_ref[s] == 1)
        def _(s=s):
            for cp in copies[s]:
                cp.wait()

            def body(k, acc):
                pair = ((z_me + k // ny) % nz) * ny + (y_me + k % ny) % ny
                a = a_v[s, k].reshape(2 * tok, BLK)
                g = g_v[s, pair].reshape(2 * tok, BLK)
                return acc + lax.dot_general(
                    a, g, (((0,), (0,)), ((), ())), preferred_element_type=jnp.float32
                )

            out_ref[s] = lax.fori_loop(
                0, chunks, body, jnp.zeros((BLK, BLK), jnp.float32), unroll=8
            )


def block_products(first, second, grad_pieces, starts, place, local_rows, local_cols, use, ny):
    chunks, tok, width = first.shape
    n_grad = len(grad_pieces)
    smem = pl.BlockSpec(memory_space=pltpu.SMEM)
    hbm = pl.BlockSpec(memory_space=pl.ANY)
    tokens = 2 * chunks * tok
    flops = 2 * MAXB * tokens * BLK * BLK
    moved = 2 * MAXB * tokens * BLK * 2 + MAXB * BLK * BLK * 4
    return pl.pallas_call(
        functools.partial(block_kernel, n_grad, ny),
        out_shape=jax.ShapeDtypeStruct((MAXB, BLK, BLK), jnp.float32),
        in_specs=[smem] * 5 + [hbm] * (2 + n_grad),
        out_specs=pl.BlockSpec(memory_space=pltpu.VMEM),
        scratch_shapes=[
            pltpu.VMEM((MAXB, chunks, 2, tok, BLK), jnp.bfloat16),
            pltpu.VMEM((MAXB, chunks, 2, tok, BLK), jnp.bfloat16),
            pltpu.SemaphoreType.DMA((MAXB, 2 + n_grad)),
        ],
        compiler_params=pltpu.CompilerParams(vmem_limit_bytes=48 * 1024 * 1024),
        cost_estimate=pl.CostEstimate(flops=flops, bytes_accessed=moved, transcendentals=0),
    )(local_rows, local_cols, use, starts, place, first, second, *grad_pieces)


def relative_gather(x, axis, n, split=True):
    right = [(k, (k + 1) % n) for k in range(n)]
    left = [(k, (k - 1) % n) for k in range(n)]
    rel = [x] + [None] * (n - 1)
    from_left, from_right = x, x
    for t in range(1, (n + 1) // 2):
        from_left = lax.ppermute(from_left, axis, right)
        from_right = lax.ppermute(from_right, axis, left)
        rel[n - t] = from_left
        rel[t] = from_right
    if n % 2 == 0 and n > 1 and not split:
        rel[n // 2] = lax.ppermute(from_left, axis, right)
    elif n % 2 == 0 and n > 1:
        t = n // 2
        half = x.shape[0] // 2
        near_a = lax.ppermute(from_left[:half], axis, right)
        near_b = lax.ppermute(from_right[half:], axis, left)
        rel[t] = jnp.concatenate([near_a, near_b], 0)
    return rel


def ring_gather(own, axis, place):
    n = lax.axis_size(axis)
    length = own.shape[0]
    right = [(k, (k + 1) % n) for k in range(n)]
    left = [(k, (k - 1) % n) for k in range(n)]
    pieces, starts = [own], [place * length]
    from_left, from_right = own, own
    for d in range(1, (n + 1) // 2):
        from_left = lax.ppermute(from_left, axis, right)
        from_right = lax.ppermute(from_right, axis, left)
        pieces += [from_left, from_right]
        starts += [((place - d) % n) * length, ((place + d) % n) * length]
    if n % 2 == 0 and n > 1:
        half = length // 2
        d = n // 2
        if d == 1:
            near_a, near_b = lax.ppermute(own[:half], axis, right), lax.ppermute(own[half:], axis, left)
        else:
            near_a = lax.ppermute(from_left[:half], axis, right)
            near_b = lax.ppermute(from_right[half:], axis, left)
        far = ((place + d) % n) * length
        pieces += [near_a, near_b]
        starts += [far, far + half]
    return pieces, jnp.stack(starts).astype(jnp.int32)


def on_device(activations, out_grad, block_rows, block_cols, counts):
    in_place = lax.axis_index("in")
    core = lax.axis_index("core")
    nz, ny, ncore = lax.axis_size("z"), lax.axis_size("y"), lax.axis_size("core")
    z_me, y_me = lax.axis_index("z"), lax.axis_index("y")
    out_place = (z_me * ny + y_me) * ncore + core
    tok = activations.shape[0]
    tile_rows = activations.shape[1] // BLK
    tile_cols = out_grad.shape[1] // BLK
    half_rows = tile_rows // 2
    local_rows = jnp.clip(block_rows[0, 0] - in_place * tile_rows, 0, tile_rows - 1)
    local_cols = jnp.clip(block_cols[0, 0] - out_place * tile_cols, 0, tile_cols - 1)
    live = jnp.arange(MAXB, dtype=jnp.int32) < counts[0, 0]
    mine_half = (local_rows // half_rows) == core
    use_mine = (live & mine_half).astype(jnp.int32)
    use_other = (live & ~mine_half).astype(jnp.int32)
    in_half = (local_rows % half_rows).astype(jnp.int32)
    place = jnp.stack([z_me, y_me]).astype(jnp.int32)

    width = half_rows * BLK
    first, second = activations[:, :width], activations[:, width:]
    on_first = core == 0
    keep = jnp.where(on_first, first, second)
    send = jnp.where(on_first, second, first)
    swap = [(0, 1), (1, 0)]
    recv = lax.ppermute(send, "core", swap)
    lead = jnp.where(on_first, keep, recv)
    trail = jnp.where(on_first, recv, keep)

    lead_z = jnp.stack(relative_gather(lead, "z", nz, split=False), 0)
    lead_all = jnp.stack(relative_gather(lead_z, "y", ny), 1)
    trail_y = jnp.stack(relative_gather(trail, "y", ny, split=False), 0)
    trail_all = jnp.stack(relative_gather(trail_y, "z", nz), 0)
    lead_all = lead_all.reshape(nz * ny, tok, width)
    trail_all = trail_all.reshape(nz * ny, tok, width)

    grad_pieces, starts = ring_gather(out_grad, "in", in_place)
    lead_all, grad_pieces = lax.optimization_barrier((lead_all, grad_pieces))
    grad_pieces = [g.reshape(g.shape[0] // (2 * tok), 2, tok, g.shape[1]) for g in grad_pieces]
    starts = starts // (2 * tok)
    lead_other = lax.ppermute(lead_all, "core", swap)
    trail_other = lax.ppermute(trail_all, "core", swap)
    part_mine = block_products(
        lead_all, trail_all, grad_pieces, starts, place, in_half, local_cols, use_mine, ny
    )
    part_other = block_products(
        lead_other, trail_other, grad_pieces, starts, place, in_half, local_cols, use_other, ny
    )
    totals = part_mine + part_other
    return totals.reshape(1, 1, MAXB, BLK, BLK)


def solution(mesh):
    n_in, n_out = mesh.devices.shape
    row = mesh.devices[0]
    ny = len({d.coords[1] for d in row})
    ncore = n_out // len({tuple(d.coords) for d in row})
    nz = n_out // (ny * ncore)
    split = jax.sharding.Mesh(
        mesh.devices.reshape(n_in, nz, ny, ncore), ("in", "z", "y", "core")
    )
    out = ("z", "y", "core")
    return jax.shard_map(
        on_device,
        mesh=split,
        in_specs=(
            P(out, "in"),
            P("in", out),
            P("in", out, None),
            P("in", out, None),
            P("in", out),
        ),
        out_specs=P("in", out, None, None, None),
        check_vma=False,
    )
```

```python
import functools

import jax
import jax.numpy as jnp
from jax import lax
from jax.experimental import pallas as pl
from jax.experimental.pallas import tpu as pltpu
from jax.sharding import PartitionSpec as P

BLK = 128
MAXB = 4


def block_kernel(n_grad, ny, rows_ref, cols_ref, use_ref, starts_ref, place_ref, *rest):
    first_hbm, second_hbm = rest[0], rest[1]
    grad_hbm = rest[2:2 + n_grad]
    out_ref, a_v, g_v, sems = rest[2 + n_grad:]
    chunks, _, tok, _ = a_v.shape[1:]

    copies = []
    for s in range(MAXB):
        r = pl.multiple_of(rows_ref[s] * BLK, BLK)
        c = pl.multiple_of(cols_ref[s] * BLK, BLK)
        slot = [
            pltpu.make_async_copy(first_hbm.at[:, :, pl.ds(r, BLK)], a_v.at[s, :, 0], sems.at[s, 0]),
            pltpu.make_async_copy(second_hbm.at[:, :, pl.ds(r, BLK)], a_v.at[s, :, 1], sems.at[s, 1]),
        ]
        for p, piece in enumerate(grad_hbm):
            slot.append(
                pltpu.make_async_copy(
                    piece.at[:, :, :, pl.ds(c, BLK)],
                    g_v.at[s, pl.ds(starts_ref[p], piece.shape[0])],
                    sems.at[s, p + 2],
                )
            )

        @pl.when(use_ref[s] == 1)
        def _(slot=slot):
            for cp in slot:
                cp.start()

        copies.append(slot)

    z_me, y_me = place_ref[0], place_ref[1]
    nz = chunks // ny
    for s in range(MAXB):

        @pl.when(use_ref[s] == 0)
        def _(s=s):
            out_ref[s] = jnp.zeros((BLK, BLK), jnp.float32)

        @pl.when(use_ref[s] == 1)
        def _(s=s):
            for cp in copies[s]:
                cp.wait()

            def body(k, acc):
                pair = ((z_me + k // ny) % nz) * ny + (y_me + k % ny) % ny
                a = a_v[s, k].reshape(2 * tok, BLK)
                g = g_v[s, pair].reshape(2 * tok, BLK)
                return acc + lax.dot_general(
                    a, g, (((0,), (0,)), ((), ())), preferred_element_type=jnp.float32
                )

            out_ref[s] = lax.fori_loop(
                0, chunks, body, jnp.zeros((BLK, BLK), jnp.float32), unroll=8
            )


def block_products(first, second, grad_pieces, starts, place, local_rows, local_cols, use, ny):
    chunks, tok, width = first.shape
    n_grad = len(grad_pieces)
    smem = pl.BlockSpec(memory_space=pltpu.SMEM)
    hbm = pl.BlockSpec(memory_space=pl.ANY)
    tokens = 2 * chunks * tok
    flops = 2 * MAXB * tokens * BLK * BLK
    moved = 2 * MAXB * tokens * BLK * 2 + MAXB * BLK * BLK * 4
    return pl.pallas_call(
        functools.partial(block_kernel, n_grad, ny),
        out_shape=jax.ShapeDtypeStruct((MAXB, BLK, BLK), jnp.float32),
        in_specs=[smem] * 5 + [hbm] * (2 + n_grad),
        out_specs=pl.BlockSpec(memory_space=pltpu.VMEM),
        scratch_shapes=[
            pltpu.VMEM((MAXB, chunks, 2, tok, BLK), jnp.bfloat16),
            pltpu.VMEM((MAXB, chunks, 2, tok, BLK), jnp.bfloat16),
            pltpu.SemaphoreType.DMA((MAXB, 2 + n_grad)),
        ],
        compiler_params=pltpu.CompilerParams(vmem_limit_bytes=48 * 1024 * 1024),
        cost_estimate=pl.CostEstimate(flops=flops, bytes_accessed=moved, transcendentals=0),
    )(local_rows, local_cols, use, starts, place, first, second, *grad_pieces)


def relative_gather(x, axis, n, split=True):
    right = [(k, (k + 1) % n) for k in range(n)]
    left = [(k, (k - 1) % n) for k in range(n)]
    rel = [x] + [None] * (n - 1)
    from_left, from_right = x, x
    for t in range(1, (n + 1) // 2):
        from_left = lax.ppermute(from_left, axis, right)
        from_right = lax.ppermute(from_right, axis, left)
        rel[n - t] = from_left
        rel[t] = from_right
    if n % 2 == 0 and n > 1 and not split:
        rel[n // 2] = lax.ppermute(from_left, axis, right)
    elif n % 2 == 0 and n > 1:
        t = n // 2
        half = x.shape[0] // 2
        near_a = lax.ppermute(from_left[:half], axis, right)
        near_b = lax.ppermute(from_right[half:], axis, left)
        rel[t] = jnp.concatenate([near_a, near_b], 0)
    return rel


def ring_gather(own, axis, place):
    n = lax.axis_size(axis)
    length = own.shape[0]
    right = [(k, (k + 1) % n) for k in range(n)]
    left = [(k, (k - 1) % n) for k in range(n)]
    pieces, starts = [own], [place * length]
    from_left, from_right = own, own
    for d in range(1, (n + 1) // 2):
        from_left = lax.ppermute(from_left, axis, right)
        from_right = lax.ppermute(from_right, axis, left)
        pieces += [from_left, from_right]
        starts += [((place - d) % n) * length, ((place + d) % n) * length]
    if n % 2 == 0 and n > 1:
        half = length // 2
        d = n // 2
        if d == 1:
            near_a, near_b = lax.ppermute(own[:half], axis, right), lax.ppermute(own[half:], axis, left)
        else:
            near_a = lax.ppermute(from_left[:half], axis, right)
            near_b = lax.ppermute(from_right[half:], axis, left)
        far = ((place + d) % n) * length
        pieces += [near_a, near_b]
        starts += [far, far + half]
    return pieces, jnp.stack(starts).astype(jnp.int32)


def on_device(activations, out_grad, block_rows, block_cols, counts):
    in_place = lax.axis_index("in")
    core = lax.axis_index("core")
    nz, ny, ncore = lax.axis_size("z"), lax.axis_size("y"), lax.axis_size("core")
    z_me, y_me = lax.axis_index("z"), lax.axis_index("y")
    out_place = (z_me * ny + y_me) * ncore + core
    tok = activations.shape[0]
    tile_rows = activations.shape[1] // BLK
    tile_cols = out_grad.shape[1] // BLK
    half_rows = tile_rows // 2
    local_rows = jnp.clip(block_rows[0, 0] - in_place * tile_rows, 0, tile_rows - 1)
    local_cols = jnp.clip(block_cols[0, 0] - out_place * tile_cols, 0, tile_cols - 1)
    live = jnp.arange(MAXB, dtype=jnp.int32) < counts[0, 0]
    mine_half = (local_rows // half_rows) == core
    use_mine = (live & mine_half).astype(jnp.int32)
    use_other = (live & ~mine_half).astype(jnp.int32)
    in_half = (local_rows % half_rows).astype(jnp.int32)
    place = jnp.stack([z_me, y_me]).astype(jnp.int32)

    width = half_rows * BLK
    first, second = activations[:, :width], activations[:, width:]
    on_first = core == 0
    keep = jnp.where(on_first, first, second)
    send = jnp.where(on_first, second, first)
    swap = [(0, 1), (1, 0)]
    recv = lax.ppermute(send, "core", swap)
    lead = jnp.where(on_first, keep, recv)
    trail = jnp.where(on_first, recv, keep)

    lead_z = jnp.stack(relative_gather(lead, "z", nz, split=False), 0)
    trail_y = jnp.stack(relative_gather(trail, "y", ny, split=False), 0)
    n_in = lax.axis_size("in")
    length = out_grad.shape[0]
    right = [(k, (k + 1) % n_in) for k in range(n_in)]
    left = [(k, (k - 1) % n_in) for k in range(n_in)]
    from_left = lax.ppermute(out_grad, "in", right)
    from_right = lax.ppermute(out_grad, "in", left)
    lead_z, trail_y, from_left, from_right = lax.optimization_barrier(
        (lead_z, trail_y, from_left, from_right)
    )
    grad_pieces = [out_grad, from_left, from_right]
    offsets = [0, -1, 1]
    for d in range(2, n_in // 2 + 1):
        from_left = lax.ppermute(from_left, "in", right)
        grad_pieces.append(from_left)
        offsets.append(-d)
        if 2 * d < n_in:
            from_right = lax.ppermute(from_right, "in", left)
            grad_pieces.append(from_right)
            offsets.append(d)
    starts = jnp.stack([((in_place + o) % n_in) * length for o in offsets]).astype(jnp.int32)
    lead_all = jnp.stack(relative_gather(lead_z, "y", ny), 1)
    trail_all = jnp.stack(relative_gather(trail_y, "z", nz), 0)
    lead_all = lead_all.reshape(nz * ny, tok, width)
    trail_all = trail_all.reshape(nz * ny, tok, width)

    lead_all, grad_pieces = lax.optimization_barrier((lead_all, grad_pieces))
    grad_pieces = [g.reshape(g.shape[0] // (2 * tok), 2, tok, g.shape[1]) for g in grad_pieces]
    starts = starts // (2 * tok)
    lead_other = lax.ppermute(lead_all, "core", swap)
    trail_other = lax.ppermute(trail_all, "core", swap)
    part_mine = block_products(
        lead_all, trail_all, grad_pieces, starts, place, in_half, local_cols, use_mine, ny
    )
    part_other = block_products(
        lead_other, trail_other, grad_pieces, starts, place, in_half, local_cols, use_other, ny
    )
    totals = part_mine + part_other
    return totals.reshape(1, 1, MAXB, BLK, BLK)


def solution(mesh):
    n_in, n_out = mesh.devices.shape
    row = mesh.devices[0]
    ny = len({d.coords[1] for d in row})
    ncore = n_out // len({tuple(d.coords) for d in row})
    nz = n_out // (ny * ncore)
    split = jax.sharding.Mesh(
        mesh.devices.reshape(n_in, nz, ny, ncore), ("in", "z", "y", "core")
    )
    out = ("z", "y", "core")
    return jax.shard_map(
        on_device,
        mesh=split,
        in_specs=(
            P(out, "in"),
            P("in", out),
            P("in", out, None),
            P("in", out, None),
            P("in", out),
        ),
        out_specs=P("in", out, None, None, None),
        check_vma=False,
    )
```
